256 devices in a mesh: tm: 8 (over y_lo, x), stn: 32 (over y_hi, z, core).
Axes of the slice: x: 4, y: 4 (y_hi: 2, y_lo: 2; y = y_hi * 2 + y_lo), z: 8, core: 2. Of those that a mesh axis runs over, the one named last changes fastest.
Arguments:
- voltages: bfloat16 [1024, 524288], P('stn', 'tm'), may hold values from -6 to 6
- gains: float32 [2, 1024, 256], P(None, 'stn'), may hold values from -4 to 4
Outputs:
- visibility: float32 [256, 2, 1024, 1024], P(('tm', 'stn'))
The draws below stay inside these ranges and needn't reach their ends.
All inputs are finite; a program needn't handle non-finite values.
Results may differ from the reference program's by a relative error of at most 0.0038.
Values may be sent and summed in bfloat16 or wider, within the bound.
No kernel may reach another device: no remote copies, remote signals or barrier semaphores. Data moves between devices by JAX's collectives and lax.ppermute only.
A program may use at most 128 MiB of HBM per device.

```python
import jax
import jax.numpy as jnp
from jax import lax

CHANNELS = 4096
BAND = 256
BAND_LOW = 1024
TAPS = 8
INPUTS = 1024
FRAMES = 64
SAMPLES = 524288


def block_levels(key, dims, shards, least, top_value):
    def one(dim, parts):
        heights = jax.random.uniform(jax.random.fold_in(jax.random.fold_in(key, 6), dim), (parts,), jnp.float32, least / len(shards), top_value / len(shards))
        return jnp.repeat(jnp.exp(heights), dims[dim] // parts).reshape((-1,) + (1,) * (len(dims) - dim - 1))

    level = one(*shards[0])
    for cut in shards[1:]:
        level = level * one(*cut)
    return level


def normal_values(rng, dims, deviation, reach, pieces=(), held_as=jnp.bfloat16):
    level = block_levels(rng, dims, pieces, -0.22, 0.18) if pieces else 1.0
    entries = jax.random.normal(rng, dims, jnp.float32) * deviation * level
    return jnp.minimum(jnp.maximum(entries, -reach), reach).astype(held_as)


def setup_inputs(seed: int = 0) -> dict:
    seeds = jax.random.split(jax.random.key(seed), 3)
    voltages = normal_values(seeds[0], (INPUTS, SAMPLES), 1.0, 6.0, ((0, 32), (1, 8)))
    gains = normal_values(seeds[1], (2, INPUTS, BAND), 0.7, 4.0, ((1, 32),), jnp.float32)
    return dict(voltages=voltages, gains=gains)


def window_table(chans):
    frame_len = 2 * chans
    total_len = TAPS * frame_len
    positions = jnp.arange(total_len, dtype=jnp.float32)
    centred = (positions - (total_len - 1) / 2.0) / frame_len
    taper = jnp.sin(jnp.pi * (positions + 0.5) / total_len)
    shaped = jnp.sinc(centred) * taper * taper
    shaped = shaped / jnp.sqrt(jnp.sum(shaped * shaped))
    return shaped.reshape(TAPS, frame_len)

def reference(voltages, gains):
    frame_len = 2 * CHANNELS
    window = window_table(CHANNELS)

    def one_input(operands):
        row_data, gain_rows = operands
        padded = jnp.concatenate([jnp.zeros(((TAPS - 1) * frame_len,), row_data.dtype), row_data])
        framed = padded.reshape(FRAMES + TAPS - 1, frame_len).astype(jnp.float32)
        windowed = jnp.zeros((FRAMES, frame_len), jnp.float32)
        for tap_index in range(TAPS):
            windowed = windowed + window[tap_index] * framed[tap_index:tap_index + FRAMES]
        spectrum = jnp.fft.rfft(windowed, axis=1)[:, BAND_LOW:BAND_LOW + BAND]
        real_part = jnp.real(spectrum).astype(jnp.float32)
        imag_part = jnp.imag(spectrum).astype(jnp.float32)
        gain_real = gain_rows[0][None, :]
        gain_imag = gain_rows[1][None, :]
        scaled_real = gain_real * real_part - gain_imag * imag_part
        scaled_imag = gain_real * imag_part + gain_imag * real_part
        return jnp.stack([scaled_real, scaled_imag]).astype(jnp.bfloat16)
    spectra = lax.map(one_input, (voltages, jnp.transpose(gains, (1, 0, 2))))
    block = min(16, BAND)
    starts = (jnp.arange(BAND // block) * block).astype(jnp.int32)

    def one_block(start):
        piece = lax.dynamic_slice_in_dim(spectra, start, block, 3).astype(jnp.float32)
        real_part = piece[:, 0]
        imag_part = piece[:, 1]
        vis_real = jnp.einsum('ifc,jfc->cij', real_part, real_part) + jnp.einsum('ifc,jfc->cij', imag_part, imag_part)
        vis_imag = jnp.einsum('ifc,jfc->cij', imag_part, real_part) - jnp.einsum('ifc,jfc->cij', real_part, imag_part)
        return jnp.stack([vis_real, vis_imag], axis=1) / FRAMES
    blocks_out = lax.map(one_block, starts)
    return blocks_out.reshape(BAND, 2, INPUTS, INPUTS)
```

```python
import numpy as np

import jax
import jax.numpy as jnp
from jax import lax
from jax.sharding import PartitionSpec as P

CHANNELS = 4096
BAND_LOW = 1024
TAPS = 8


def passed_along(x, axis, by):
    devices = lax.axis_size(axis)
    pairs = [(i, i + by) for i in range(devices) if 0 <= i + by < devices]
    return lax.ppermute(x, axis, pairs)


def window_table(chans):
    frame_len = 2 * chans
    total_len = TAPS * frame_len
    positions = np.arange(total_len, dtype=np.float64)
    centred = (positions - (total_len - 1) / 2.0) / frame_len
    taper = np.sin(np.pi * (positions + 0.5) / total_len)
    shaped = np.sinc(centred) * taper * taper
    shaped = shaped / np.sqrt(np.sum(shaped * shaped))
    return shaped.reshape(TAPS, frame_len).astype(np.float32)


def split(x):
    hi = lax.reduce_precision(x, exponent_bits=8, mantissa_bits=7)
    lo = x - hi
    return hi.astype(jnp.bfloat16), lo.astype(jnp.bfloat16)


def band_tables(frame_len, band):
    half = band // 2
    n_b = 32
    n_a = frame_len // 2 // n_b
    q = jnp.arange(2, dtype=jnp.int32)[:, None, None]
    k = jnp.arange(band, dtype=jnp.int32)[None, None, :]
    chan = 2 * (k % half) + q
    imag_col = k >= half
    a = jnp.arange(n_a, dtype=jnp.int32)[None, :, None]
    b = jnp.arange(n_b, dtype=jnp.int32)[None, :, None]
    p_steps = n_a * 2
    tp = (2.0 * jnp.pi / p_steps) * ((a * chan) % p_steps).astype(jnp.float32)
    tq = (2.0 * jnp.pi / frame_len) * ((b * (BAND_LOW + chan)) % frame_len).astype(jnp.float32)
    pr, pi = jnp.cos(tp), -jnp.sin(tp)
    qr, qi = jnp.cos(tq), -jnp.sin(tq)
    b1 = jnp.where(imag_col, qi, qr)
    b2 = jnp.where(imag_col, qr, -qi)
    t = pr[:, :, None, :] * b1[:, None, :, :] + pi[:, :, None, :] * b2[:, None, :, :]
    return split(t.reshape(2, n_a * n_b, band))


def on_device(voltages, gains):
    in_dev, length = voltages.shape
    band = gains.shape[2]
    half_band = band // 2
    frame_len = 2 * CHANNELS
    half_len = frame_len // 2
    frames = length // frame_len
    n_time = lax.axis_size("tm")
    n_station = lax.axis_size("stn")
    all_inputs = in_dev * n_station
    history = TAPS - 1
    slots = frames + history
    window = jnp.asarray(window_table(CHANNELS))
    t_hi, t_lo = band_tables(frame_len, band)

    framed = voltages.reshape(in_dev, frames, frame_len)
    pad = jnp.zeros((in_dev, history, frame_len), voltages.dtype)
    padded = jnp.concatenate([pad, framed, pad], axis=1).astype(jnp.float32)
    windowed = window[0] * padded[:, 0:slots, :]
    for tap_index in range(1, TAPS):
        windowed = windowed + window[tap_index] * padded[:, tap_index : tap_index + slots, :]
    first, second = windowed[..., :half_len], windowed[..., half_len:]
    folded = jnp.stack([first + second, first - second])
    l_hi, l_lo = split(folded)
    lhs = jnp.stack([l_hi, l_lo], axis=1)
    f32 = jnp.float32
    part_hi = jnp.einsum("qhism,qmk->qhisk", lhs, t_hi, preferred_element_type=f32)
    part_lo = jnp.einsum("qism,qmk->qisk", l_hi, t_lo, preferred_element_type=f32)
    raw = (part_hi[:, 0] + part_hi[:, 1]) + part_lo

    own = raw[:, :, :frames, :]
    given = passed_along(raw[:, :, frames:, :], "tm", 1)
    own = own.at[:, :, :history, :].add(given)

    own = own.reshape(2, in_dev, frames, 2, half_band)
    raw_re = jnp.transpose(own[:, :, :, 0, :], (3, 0, 1, 2))
    raw_im = jnp.transpose(own[:, :, :, 1, :], (3, 0, 1, 2))
    g = jnp.transpose(gains.reshape(2, in_dev, half_band, 2), (0, 2, 3, 1))[..., None]
    gain_re, gain_im = g[0], g[1]
    spec_re = gain_re * raw_re - gain_im * raw_im
    spec_im = gain_re * raw_im + gain_im * raw_re
    spectra = jnp.stack([spec_re, spec_im], axis=3).astype(jnp.bfloat16)
    row = in_dev * 2 * frames
    spectra = spectra.reshape(n_time, n_station, row)
    spectra = lax.all_to_all(spectra, "tm", split_axis=0, concat_axis=0, tiled=True)
    spectra = lax.all_to_all(spectra, "stn", split_axis=1, concat_axis=1, tiled=True)
    spectra = spectra.reshape(n_time, n_station, in_dev, 2, frames)
    spectra = jnp.transpose(spectra, (1, 2, 3, 0, 4)).reshape(all_inputs, 2, n_time * frames)
    stacked = spectra.reshape(all_inputs, 2 * n_time * frames)
    flipped = jnp.concatenate([spectra[:, 1], -spectra[:, 0]], axis=-1)
    both = jnp.concatenate([stacked, flipped], axis=0)
    vis = jnp.einsum("ik,jk->ij", both, stacked, preferred_element_type=f32)
    vis = vis * (1.0 / float(n_time * frames))
    return vis.reshape(1, 2, all_inputs, all_inputs)


def solution(mesh):
    in_specs = (P("stn", "tm"), P(None, "stn", None))
    out_specs = P(("tm", "stn"), None, None, None)
    return jax.shard_map(
        on_device, mesh=mesh, in_specs=in_specs, out_specs=out_specs, check_vma=False
    )
```

```python
import numpy as np

import jax
import jax.numpy as jnp
from jax import lax
from jax.experimental import pallas as pl
from jax.experimental.pallas import tpu as pltpu
from jax.sharding import PartitionSpec as P

CHANNELS = 4096
BAND_LOW = 1024
TAPS = 8


def passed_along(x, axis, by):
    devices = lax.axis_size(axis)
    pairs = [(i, i + by) for i in range(devices) if 0 <= i + by < devices]
    return lax.ppermute(x, axis, pairs)


def window_table(chans):
    frame_len = 2 * chans
    total_len = TAPS * frame_len
    positions = np.arange(total_len, dtype=np.float64)
    centred = (positions - (total_len - 1) / 2.0) / frame_len
    taper = np.sin(np.pi * (positions + 0.5) / total_len)
    shaped = np.sinc(centred) * taper * taper
    shaped = shaped / np.sqrt(np.sum(shaped * shaped))
    return shaped.reshape(TAPS, frame_len).astype(np.float32)


def split(x):
    hi = lax.reduce_precision(x, exponent_bits=8, mantissa_bits=7)
    lo = x - hi
    return hi.astype(jnp.bfloat16), lo.astype(jnp.bfloat16)


def band_tables(frame_len, band):
    half = band // 2
    n_b = 32
    n_a = frame_len // 2 // n_b
    q = jnp.arange(2, dtype=jnp.int32)[:, None, None]
    k = jnp.arange(band, dtype=jnp.int32)[None, None, :]
    chan = 2 * (k % half) + q
    imag_col = k >= half
    a = jnp.arange(n_a, dtype=jnp.int32)[None, :, None]
    b = jnp.arange(n_b, dtype=jnp.int32)[None, :, None]
    p_steps = n_a * 2
    tp = (2.0 * jnp.pi / p_steps) * ((a * chan) % p_steps).astype(jnp.float32)
    tq = (2.0 * jnp.pi / frame_len) * ((b * (BAND_LOW + chan)) % frame_len).astype(jnp.float32)
    pr, pi = jnp.cos(tp), -jnp.sin(tp)
    qr, qi = jnp.cos(tq), -jnp.sin(tq)
    b1 = jnp.where(imag_col, qi, qr)
    b2 = jnp.where(imag_col, qr, -qi)
    t = pr[:, :, None, :] * b1[:, None, :, :] + pi[:, :, None, :] * b2[:, None, :, :]
    return split(t.reshape(2, n_a * n_b, band))


def taps_kernel(x_ref, w_ref, own_ref, next_ref):
    frame_len = w_ref.shape[1]
    half = frame_len // 2
    frames = x_ref.shape[1] // frame_len
    history = TAPS - 1
    lanes = 128

    def chunk(j, carry):
        base = pl.multiple_of(j * lanes, lanes)
        xs = []
        ws = []
        for offset in (0, half):
            xs.append([x_ref[:, pl.ds(f * frame_len + offset + base, lanes)].astype(jnp.float32) for f in range(frames)])
            ws.append([w_ref[pl.ds(p, 1), pl.ds(offset + base, lanes)] for p in range(TAPS)])
        for s in range(frames + history):
            accs = []
            for part in range(2):
                acc = None
                for p in range(TAPS):
                    g = s + p - history
                    if 0 <= g < frames:
                        term = ws[part][p] * xs[part][g]
                        acc = term if acc is None else acc + term
                accs.append(acc)
            folded = (accs[0] + accs[1], accs[0] - accs[1])
            ref, slot = (own_ref, s) if s < frames else (next_ref, s - frames)
            for q in range(2):
                hi = folded[q].astype(jnp.bfloat16)
                lo = (folded[q] - hi.astype(jnp.float32)).astype(jnp.bfloat16)
                ref[q, 0, slot, :, pl.ds(base, lanes)] = hi
                ref[q, 1, slot, :, pl.ds(base, lanes)] = lo
        return carry

    lax.fori_loop(0, half // lanes, chunk, 0)


def windowed_parts(voltages, window, frames):
    in_dev, length = voltages.shape
    frame_len = window.shape[1]
    half = frame_len // 2
    history = TAPS - 1
    block = 16
    out_shape = (
        jax.ShapeDtypeStruct((2, 2, frames, in_dev, half), jnp.bfloat16),
        jax.ShapeDtypeStruct((2, 2, history, in_dev, half), jnp.bfloat16),
    )
    return pl.pallas_call(
        taps_kernel,
        out_shape=out_shape,
        grid=(in_dev // block,),
        in_specs=[
            pl.BlockSpec((block, length), lambda g: (g, 0)),
            pl.BlockSpec((TAPS, frame_len), lambda g: (0, 0)),
        ],
        out_specs=[
            pl.BlockSpec((2, 2, frames, block, half), lambda g: (0, 0, 0, g, 0)),
            pl.BlockSpec((2, 2, history, block, half), lambda g: (0, 0, 0, g, 0)),
        ],
        compiler_params=pltpu.CompilerParams(vmem_limit_bytes=48 * 1024 * 1024),
    )(voltages, window)


def band_dft(parts, t_hi, t_lo):
    q, h, slots, inputs, m = parts.shape
    lhs = parts.reshape(q, h, slots * inputs, m)
    f32 = jnp.float32
    both = jnp.einsum("qhrm,qmk->qhkr", lhs, t_hi, preferred_element_type=f32)
    high = jnp.einsum("qrm,qmk->qkr", lhs[:, 0], t_lo, preferred_element_type=f32)
    return (both[:, 0] + both[:, 1]) + high


def on_device(voltages, gains):
    in_dev, length = voltages.shape
    band = gains.shape[2]
    half_band = band // 2
    frame_len = 2 * CHANNELS
    frames = length // frame_len
    n_time = lax.axis_size("tm")
    n_station = lax.axis_size("stn")
    all_inputs = in_dev * n_station
    history = TAPS - 1
    window = jnp.asarray(window_table(CHANNELS))
    t_hi, t_lo = band_tables(frame_len, band)

    own_parts, next_parts = windowed_parts(voltages, window, frames)
    raw_next = band_dft(next_parts, t_hi, t_lo)
    given = passed_along(raw_next, "tm", 1)
    raw = band_dft(own_parts, t_hi, t_lo)
    raw = raw.at[:, :, : history * in_dev].add(given)

    row = frames * in_dev
    raw = jnp.transpose(raw.reshape(2, 2, half_band, row), (1, 2, 0, 3))
    raw_re, raw_im = raw[0], raw[1]
    g = jnp.transpose(gains.reshape(2, in_dev, half_band, 2), (0, 2, 3, 1))
    g = jnp.tile(g, (1, 1, 1, frames))
    gain_re, gain_im = g[0], g[1]
    spec_re = gain_re * raw_re - gain_im * raw_im
    spec_im = gain_re * raw_im + gain_im * raw_re
    spectra = jnp.stack([spec_re, spec_im], axis=2).astype(jnp.bfloat16)
    spectra = spectra.reshape(n_time * n_station, 2 * row)
    spectra = lax.all_to_all(spectra, ("tm", "stn"), split_axis=0, concat_axis=0, tiled=True)
    spectra = spectra.reshape(n_time, n_station, 2, frames, in_dev)
    stacked = jnp.transpose(spectra, (2, 0, 3, 1, 4)).reshape(2, n_time * frames, all_inputs)
    flipped = jnp.concatenate([stacked[1], -stacked[0]], axis=0)
    stacked = stacked.reshape(2 * n_time * frames, all_inputs)
    both = jnp.concatenate([stacked, flipped], axis=1)
    vis = jnp.einsum("ki,kj->ij", both, stacked, preferred_element_type=jnp.float32)
    vis = vis * (1.0 / float(n_time * frames))
    return vis.reshape(1, 2, all_inputs, all_inputs)


def solution(mesh):
    in_specs = (P("stn", "tm"), P(None, "stn", None))
    out_specs = P(("tm", "stn"), None, None, None)
    return jax.shard_map(
        on_device, mesh=mesh, in_specs=in_specs, out_specs=out_specs, check_vma=False
    )
```

```python
import functools

import numpy as np

import jax
import jax.numpy as jnp
from jax import lax
from jax.experimental import pallas as pl
from jax.experimental.pallas import tpu as pltpu
from jax.sharding import PartitionSpec as P

CHANNELS = 4096
BAND_LOW = 1024
TAPS = 8


def passed_along(x, axis, by):
    devices = lax.axis_size(axis)
    pairs = [(i, i + by) for i in range(devices) if 0 <= i + by < devices]
    return lax.ppermute(x, axis, pairs)


def window_table(chans):
    frame_len = 2 * chans
    total_len = TAPS * frame_len
    positions = np.arange(total_len, dtype=np.float64)
    centred = (positions - (total_len - 1) / 2.0) / frame_len
    taper = np.sin(np.pi * (positions + 0.5) / total_len)
    shaped = np.sinc(centred) * taper * taper
    shaped = shaped / np.sqrt(np.sum(shaped * shaped))
    return shaped.reshape(TAPS, frame_len).astype(np.float32)


def split(x):
    hi = lax.reduce_precision(x, exponent_bits=8, mantissa_bits=7)
    lo = x - hi
    return hi.astype(jnp.bfloat16), lo.astype(jnp.bfloat16)


def band_tables(frame_len, band):
    half = band // 2
    n_b = 128
    n_a = frame_len // 2 // n_b
    q = jnp.arange(2, dtype=jnp.int32)[:, None, None]
    k = jnp.arange(band, dtype=jnp.int32)[None, :, None]
    chan = 2 * (k % half) + q
    imag_row = k >= half
    a = jnp.arange(n_a, dtype=jnp.int32)[None, None, :]
    b = jnp.arange(n_b, dtype=jnp.int32)[None, None, :]
    p_steps = frame_len // n_b
    tp = (2.0 * jnp.pi / p_steps) * ((a * chan) % p_steps).astype(jnp.float32)
    tq = (2.0 * jnp.pi / frame_len) * ((b * (BAND_LOW + chan)) % frame_len).astype(jnp.float32)
    pr, pi = jnp.cos(tp), -jnp.sin(tp)
    qr, qi = jnp.cos(tq), -jnp.sin(tq)
    b1 = jnp.where(imag_row, qi, qr)
    b2 = jnp.where(imag_row, qr, -qi)
    t = pr[..., None] * b1[:, :, None, :] + pi[..., None] * b2[:, :, None, :]
    return split(t.reshape(2, band, n_a * n_b))


def taps_dft_kernel(x_ref, w_ref, th_hbm, tl_hbm, out_ref, lhs_ref, th_ref, tl_ref, sem, *, first_slot, n_slots):
    step = pl.program_id(0)
    steps = pl.num_programs(0)
    block = x_ref.shape[0]
    inputs = block * steps
    frame_len = w_ref.shape[1]
    half = frame_len // 2
    frames = x_ref.shape[1] // frame_len
    history = TAPS - 1
    lanes = 128
    copy_hi = pltpu.make_async_copy(th_hbm, th_ref, sem.at[0])
    copy_lo = pltpu.make_async_copy(tl_hbm, tl_ref, sem.at[1])

    @pl.when(step == 0)
    def _():
        copy_hi.start()
        copy_lo.start()

    row0 = pl.multiple_of(step * block, block)

    def chunk(j, carry):
        base = pl.multiple_of(j * lanes, lanes)
        xs = []
        ws = []
        for offset in (0, half):
            xs.append([x_ref[:, pl.ds(f * frame_len + offset + base, lanes)].astype(jnp.float32) for f in range(frames)])
            ws.append([w_ref[pl.ds(p, 1), pl.ds(offset + base, lanes)] for p in range(TAPS)])
        for slot in range(n_slots):
            s = first_slot + slot
            accs = []
            for part in range(2):
                acc = None
                for p in range(TAPS):
                    g = s + p - history
                    if 0 <= g < frames:
                        term = ws[part][p] * xs[part][g]
                        acc = term if acc is None else acc + term
                accs.append(acc)
            folded = (accs[0] + accs[1], accs[0] - accs[1])
            rows = pl.ds(pl.multiple_of(slot * inputs + row0, block), block)
            for q in range(2):
                hi = folded[q].astype(jnp.bfloat16)
                lo = (folded[q] - hi.astype(jnp.float32)).astype(jnp.bfloat16)
                lhs_ref[q, 0, rows, pl.ds(base, lanes)] = hi
                lhs_ref[q, 1, rows, pl.ds(base, lanes)] = lo
        return carry

    lax.fori_loop(0, half // lanes, chunk, 0)

    @pl.when(step == steps - 1)
    def _():
        copy_hi.wait()
        copy_lo.wait()
        depth = 512
        nt = (((1,), (1,)), ((), ()))
        f32 = jnp.float32
        for q in range(2):
            out_ref[q] = jnp.zeros(out_ref.shape[1:], f32)

            def kstep(kk, carry):
                k0 = pl.multiple_of(kk * depth, depth)
                cols = pl.ds(k0, depth)
                hi = lhs_ref[q, 0, :, cols]
                lo = lhs_ref[q, 1, :, cols]
                t_hi = th_ref[q, :, cols]
                t_lo = tl_ref[q, :, cols]
                acc = lax.dot_general(t_hi, hi, nt, preferred_element_type=f32)
                acc = acc + lax.dot_general(t_hi, lo, nt, preferred_element_type=f32)
                acc = acc + lax.dot_general(t_lo, hi, nt, preferred_element_type=f32)
                out_ref[q] += acc
                return carry

            lax.fori_loop(0, half // depth, kstep, 0)


def band_spectra(voltages, window, t_hi, t_lo, frames, first_slot, n_slots):
    in_dev, length = voltages.shape
    frame_len = window.shape[1]
    half = frame_len // 2
    band = t_hi.shape[1]
    block = 16
    rows = n_slots * in_dev
    kernel = functools.partial(taps_dft_kernel, first_slot=first_slot, n_slots=n_slots)
    return pl.pallas_call(
        kernel,
        out_shape=jax.ShapeDtypeStruct((2, band, rows), jnp.float32),
        grid=(in_dev // block,),
        in_specs=[
            pl.BlockSpec((block, length), lambda g: (g, 0)),
            pl.BlockSpec((TAPS, frame_len), lambda g: (0, 0)),
            pl.BlockSpec(memory_space=pl.ANY),
            pl.BlockSpec(memory_space=pl.ANY),
        ],
        out_specs=pl.BlockSpec((2, band, rows), lambda g: (0, 0, 0)),
        scratch_shapes=[
            pltpu.VMEM((2, 2, rows, half), jnp.bfloat16),
            pltpu.VMEM((2, band, half), jnp.bfloat16),
            pltpu.VMEM((2, band, half), jnp.bfloat16),
            pltpu.SemaphoreType.DMA((2,)),
        ],
        compiler_params=pltpu.CompilerParams(vmem_limit_bytes=48 * 1024 * 1024),
    )(voltages, window, t_hi, t_lo)


def on_device(voltages, gains):
    in_dev, length = voltages.shape
    band = gains.shape[2]
    half_band = band // 2
    frame_len = 2 * CHANNELS
    frames = length // frame_len
    n_time = lax.axis_size("tm")
    n_station = lax.axis_size("stn")
    all_inputs = in_dev * n_station
    history = TAPS - 1
    window = jnp.asarray(window_table(CHANNELS))
    t_hi, t_lo = band_tables(frame_len, band)

    raw_next = band_spectra(voltages, window, t_hi, t_lo, frames, frames, history)
    given = passed_along(raw_next, "tm", 1)
    raw = band_spectra(voltages, window, t_hi, t_lo, frames, 0, frames)
    raw = raw.at[:, :, : history * in_dev].add(given)

    row = frames * in_dev
    raw = jnp.transpose(raw.reshape(2, 2, half_band, row), (1, 2, 0, 3))
    raw_re, raw_im = raw[0], raw[1]
    g = jnp.transpose(gains.reshape(2, in_dev, half_band, 2), (0, 2, 3, 1))
    g = jnp.tile(g, (1, 1, 1, frames))
    gain_re, gain_im = g[0], g[1]
    spec_re = gain_re * raw_re - gain_im * raw_im
    spec_im = gain_re * raw_im + gain_im * raw_re
    spectra = jnp.stack([spec_re, spec_im], axis=2).astype(jnp.bfloat16)
    spectra = spectra.reshape(n_time * n_station, 2 * row)
    spectra = lax.all_to_all(spectra, ("tm", "stn"), split_axis=0, concat_axis=0, tiled=True)
    spectra = spectra.reshape(n_time, n_station, 2, frames, in_dev)
    stacked = jnp.transpose(spectra, (2, 0, 3, 1, 4)).reshape(2, n_time * frames, all_inputs)
    flipped = jnp.concatenate([stacked[1], -stacked[0]], axis=0)
    stacked = stacked.reshape(2 * n_time * frames, all_inputs)
    both = jnp.concatenate([stacked, flipped], axis=1)
    vis = jnp.einsum("ki,kj->ij", both, stacked, preferred_element_type=jnp.float32)
    vis = vis * (1.0 / float(n_time * frames))
    return vis.reshape(1, 2, all_inputs, all_inputs)


def solution(mesh):
    in_specs = (P("stn", "tm"), P(None, "stn", None))
    out_specs = P(("tm", "stn"), None, None, None)
    return jax.shard_map(
        on_device, mesh=mesh, in_specs=in_specs, out_specs=out_specs, check_vma=False
    )
```

```python
import functools

import numpy as np

import jax
import jax.numpy as jnp
from jax import lax
from jax.experimental import pallas as pl
from jax.experimental.pallas import tpu as pltpu
from jax.sharding import PartitionSpec as P

CHANNELS = 4096
BAND_LOW = 1024
TAPS = 8


def passed_along(x, axis, by):
    devices = lax.axis_size(axis)
    pairs = [(i, i + by) for i in range(devices) if 0 <= i + by < devices]
    return lax.ppermute(x, axis, pairs)


def window_table(chans):
    frame_len = 2 * chans
    total_len = TAPS * frame_len
    positions = np.arange(total_len, dtype=np.float64)
    centred = (positions - (total_len - 1) / 2.0) / frame_len
    taper = np.sin(np.pi * (positions + 0.5) / total_len)
    shaped = np.sinc(centred) * taper * taper
    shaped = shaped / np.sqrt(np.sum(shaped * shaped))
    return shaped.reshape(TAPS, frame_len).astype(np.float32)


def split(x):
    hi = lax.reduce_precision(x, exponent_bits=8, mantissa_bits=7)
    lo = x - hi
    return hi.astype(jnp.bfloat16), lo.astype(jnp.bfloat16)


def band_tables(frame_len, band):
    half = band // 2
    n_b = 32
    n_a = frame_len // 2 // n_b
    q = jnp.arange(2, dtype=jnp.int32)[:, None, None]
    k = jnp.arange(band, dtype=jnp.int32)[None, None, :]
    chan = 2 * (k % half) + q
    imag_col = k >= half
    a = jnp.arange(n_a, dtype=jnp.int32)[None, :, None]
    b = jnp.arange(n_b, dtype=jnp.int32)[None, :, None]
    p_steps = n_a * 2
    tp = (2.0 * jnp.pi / p_steps) * ((a * chan) % p_steps).astype(jnp.float32)
    tq = (2.0 * jnp.pi / frame_len) * ((b * (BAND_LOW + chan)) % frame_len).astype(jnp.float32)
    pr, pi = jnp.cos(tp), -jnp.sin(tp)
    qr, qi = jnp.cos(tq), -jnp.sin(tq)
    b1 = jnp.where(imag_col, qi, qr)
    b2 = jnp.where(imag_col, qr, -qi)
    t = pr[:, :, None, :] * b1[:, None, :, :] + pi[:, :, None, :] * b2[:, None, :, :]
    return split(t.reshape(2, n_a * n_b, band))


def taps_dft_kernel(x_ref, w_ref, th_hbm, tl_hbm, out_ref, lhs_ref, th_ref, tl_ref, sem, *, first_slot, n_slots):
    step = pl.program_id(0)
    steps = pl.num_programs(0)
    block = x_ref.shape[0]
    inputs = block * steps
    frame_len = w_ref.shape[1]
    half = frame_len // 2
    frames = x_ref.shape[1] // frame_len
    history = TAPS - 1
    lanes = 128
    copy_hi = pltpu.make_async_copy(th_hbm, th_ref, sem.at[0])
    copy_lo = pltpu.make_async_copy(tl_hbm, tl_ref, sem.at[1])

    @pl.when(step == 0)
    def _():
        copy_hi.start()
        copy_lo.start()

    row0 = pl.multiple_of(step * block, block)

    def chunk(j, carry):
        base = pl.multiple_of(j * lanes, lanes)
        xs = []
        ws = []
        for offset in (0, half):
            xs.append([x_ref[:, pl.ds(f * frame_len + offset + base, lanes)].astype(jnp.float32) for f in range(frames)])
            ws.append([w_ref[pl.ds(p, 1), pl.ds(offset + base, lanes)] for p in range(TAPS)])
        for slot in range(n_slots):
            s = first_slot + slot
            accs = []
            for part in range(2):
                acc = None
                for p in range(TAPS):
                    g = s + p - history
                    if 0 <= g < frames:
                        term = ws[part][p] * xs[part][g]
                        acc = term if acc is None else acc + term
                accs.append(acc)
            folded = (accs[0] + accs[1], accs[0] - accs[1])
            rows = pl.ds(pl.multiple_of(slot * inputs + row0, block), block)
            for q in range(2):
                hi = folded[q].astype(jnp.bfloat16)
                lo = (folded[q] - hi.astype(jnp.float32)).astype(jnp.bfloat16)
                lhs_ref[q, 0, rows, pl.ds(base, lanes)] = hi
                lhs_ref[q, 1, rows, pl.ds(base, lanes)] = lo
        return carry

    lax.fori_loop(0, half // lanes, chunk, 0)

    @pl.when(step == steps - 1)
    def _():
        copy_hi.wait()
        copy_lo.wait()
        depth = 512
        f32 = jnp.float32
        for q in range(2):
            out_ref[q] = jnp.zeros(out_ref.shape[1:], f32)

            def kstep(kk, carry):
                k0 = pl.multiple_of(kk * depth, depth)
                cols = pl.ds(k0, depth)
                hi = lhs_ref[q, 0, :, cols]
                lo = lhs_ref[q, 1, :, cols]
                t_hi = th_ref[q, cols, :]
                t_lo = tl_ref[q, cols, :]
                acc = jnp.dot(hi, t_hi, preferred_element_type=f32)
                acc = acc + jnp.dot(lo, t_hi, preferred_element_type=f32)
                acc = acc + jnp.dot(hi, t_lo, preferred_element_type=f32)
                out_ref[q] += acc
                return carry

            lax.fori_loop(0, half // depth, kstep, 0)


def band_spectra(voltages, window, t_hi, t_lo, frames, first_slot, n_slots):
    in_dev, length = voltages.shape
    frame_len = window.shape[1]
    half = frame_len // 2
    band = t_hi.shape[2]
    block = 16
    rows = n_slots * in_dev
    kernel = functools.partial(taps_dft_kernel, first_slot=first_slot, n_slots=n_slots)
    return pl.pallas_call(
        kernel,
        out_shape=jax.ShapeDtypeStruct((2, rows, band), jnp.float32),
        grid=(in_dev // block,),
        in_specs=[
            pl.BlockSpec((block, length), lambda g: (g, 0)),
            pl.BlockSpec((TAPS, frame_len), lambda g: (0, 0)),
            pl.BlockSpec(memory_space=pl.ANY),
            pl.BlockSpec(memory_space=pl.ANY),
        ],
        out_specs=pl.BlockSpec((2, rows, band), lambda g: (0, 0, 0)),
        scratch_shapes=[
            pltpu.VMEM((2, 2, rows, half), jnp.bfloat16),
            pltpu.VMEM((2, half, band), jnp.bfloat16),
            pltpu.VMEM((2, half, band), jnp.bfloat16),
            pltpu.SemaphoreType.DMA((2,)),
        ],
        compiler_params=pltpu.CompilerParams(vmem_limit_bytes=48 * 1024 * 1024),
    )(voltages, window, t_hi, t_lo)


def on_device(voltages, gains):
    in_dev, length = voltages.shape
    band = gains.shape[2]
    half_band = band // 2
    frame_len = 2 * CHANNELS
    frames = length // frame_len
    n_time = lax.axis_size("tm")
    n_station = lax.axis_size("stn")
    all_inputs = in_dev * n_station
    history = TAPS - 1
    window = jnp.asarray(window_table(CHANNELS))
    t_hi, t_lo = band_tables(frame_len, band)

    raw_next = band_spectra(voltages, window, t_hi, t_lo, frames, frames, history)
    given = passed_along(raw_next, "tm", 1)
    raw = band_spectra(voltages, window, t_hi, t_lo, frames, 0, frames)
    raw = raw.at[:, : history * in_dev, :].add(given)
    raw = jnp.transpose(raw, (0, 2, 1))

    row = frames * in_dev
    raw = jnp.transpose(raw.reshape(2, 2, half_band, row), (1, 2, 0, 3))
    raw_re, raw_im = raw[0], raw[1]
    g = jnp.transpose(gains.reshape(2, in_dev, half_band, 2), (0, 2, 3, 1))
    g = jnp.tile(g, (1, 1, 1, frames))
    gain_re, gain_im = g[0], g[1]
    spec_re = gain_re * raw_re - gain_im * raw_im
    spec_im = gain_re * raw_im + gain_im * raw_re
    spectra = jnp.stack([spec_re, spec_im], axis=2).astype(jnp.bfloat16)
    spectra = spectra.reshape(n_time * n_station, 2 * row)
    spectra = lax.all_to_all(spectra, ("tm", "stn"), split_axis=0, concat_axis=0, tiled=True)
    spectra = spectra.reshape(n_time, n_station, 2, frames, in_dev)
    stacked = jnp.transpose(spectra, (2, 0, 3, 1, 4)).reshape(2, n_time * frames, all_inputs)
    flipped = jnp.concatenate([stacked[1], -stacked[0]], axis=0)
    stacked = stacked.reshape(2 * n_time * frames, all_inputs)
    both = jnp.concatenate([stacked, flipped], axis=1)
    vis = jnp.einsum("ki,kj->ij", both, stacked, preferred_element_type=jnp.float32)
    vis = vis * (1.0 / float(n_time * frames))
    return vis.reshape(1, 2, all_inputs, all_inputs)


def solution(mesh):
    in_specs = (P("stn", "tm"), P(None, "stn", None))
    out_specs = P(("tm", "stn"), None, None, None)
    return jax.shard_map(
        on_device, mesh=mesh, in_specs=in_specs, out_specs=out_specs, check_vma=False
    )
```

```python
import functools

import numpy as np

import jax
import jax.numpy as jnp
from jax import lax
from jax.experimental import pallas as pl
from jax.experimental.pallas import tpu as pltpu
from jax.sharding import PartitionSpec as P

CHANNELS = 4096
BAND_LOW = 1024
TAPS = 8


def passed_along(x, axis, by):
    devices = lax.axis_size(axis)
    pairs = [(i, i + by) for i in range(devices) if 0 <= i + by < devices]
    return lax.ppermute(x, axis, pairs)


def window_table(chans):
    frame_len = 2 * chans
    total_len = TAPS * frame_len
    positions = np.arange(total_len, dtype=np.float64)
    centred = (positions - (total_len - 1) / 2.0) / frame_len
    taper = np.sin(np.pi * (positions + 0.5) / total_len)
    shaped = np.sinc(centred) * taper * taper
    shaped = shaped / np.sqrt(np.sum(shaped * shaped))
    return shaped.reshape(TAPS, frame_len).astype(np.float32)


def split(x):
    hi = lax.reduce_precision(x, exponent_bits=8, mantissa_bits=7)
    lo = x - hi
    return hi.astype(jnp.bfloat16), lo.astype(jnp.bfloat16)


def band_tables(frame_len, band):
    half = band // 2
    n_b = 32
    n_a = frame_len // 2 // n_b
    q = jnp.arange(2, dtype=jnp.int32)[:, None, None]
    k = jnp.arange(band, dtype=jnp.int32)[None, None, :]
    chan = 2 * (k % half) + q
    imag_col = k >= half
    a = jnp.arange(n_a, dtype=jnp.int32)[None, :, None]
    b = jnp.arange(n_b, dtype=jnp.int32)[None, :, None]
    p_steps = n_a * 2
    tp = (2.0 * jnp.pi / p_steps) * ((a * chan) % p_steps).astype(jnp.float32)
    tq = (2.0 * jnp.pi / frame_len) * ((b * (BAND_LOW + chan)) % frame_len).astype(jnp.float32)
    pr, pi = jnp.cos(tp), -jnp.sin(tp)
    qr, qi = jnp.cos(tq), -jnp.sin(tq)
    b1 = jnp.where(imag_col, qi, qr)
    b2 = jnp.where(imag_col, qr, -qi)
    t = pr[:, :, None, :] * b1[:, None, :, :] + pi[:, :, None, :] * b2[:, None, :, :]
    t = t.reshape(2, n_a * n_b, band)
    hi = lax.reduce_precision(t, exponent_bits=8, mantissa_bits=7)
    return jnp.stack([hi, t - hi]).astype(jnp.bfloat16)


def taps_dft_kernel(x_ref, w_ref, table_hbm, out_ref, lhs_ref, th_ref, tl_ref, sem, *, first_slot, n_slots):
    step = pl.program_id(0)
    steps = pl.num_programs(0)
    block = x_ref.shape[0]
    inputs = block * steps
    frame_len = w_ref.shape[1]
    half = frame_len // 2
    frames = x_ref.shape[1] // frame_len
    history = TAPS - 1
    lanes = 128
    copy_hi = pltpu.make_async_copy(table_hbm.at[0], th_ref, sem.at[0])
    copy_lo = pltpu.make_async_copy(table_hbm.at[1], tl_ref, sem.at[1])

    @pl.when(step == 0)
    def _():
        copy_hi.start()
        copy_lo.start()

    row0 = pl.multiple_of(step * block, block)

    def chunk(j, carry):
        base = pl.multiple_of(j * lanes, lanes)
        xs = []
        ws = []
        for offset in (0, half):
            xs.append([x_ref[:, pl.ds(f * frame_len + offset + base, lanes)].astype(jnp.float32) for f in range(frames)])
            ws.append([w_ref[pl.ds(p, 1), pl.ds(offset + base, lanes)] for p in range(TAPS)])
        for slot in range(n_slots):
            s = first_slot + slot
            accs = []
            for part in range(2):
                acc = None
                for p in range(TAPS):
                    g = s + p - history
                    if 0 <= g < frames:
                        term = ws[part][p] * xs[part][g]
                        acc = term if acc is None else acc + term
                accs.append(acc)
            folded = (accs[0] + accs[1], accs[0] - accs[1])
            rows = pl.ds(pl.multiple_of(slot * inputs + row0, block), block)
            for q in range(2):
                hi = folded[q].astype(jnp.bfloat16)
                lo = (folded[q] - hi.astype(jnp.float32)).astype(jnp.bfloat16)
                lhs_ref[q, 0, rows, pl.ds(base, lanes)] = hi
                lhs_ref[q, 1, rows, pl.ds(base, lanes)] = lo
        return carry

    lax.fori_loop(0, half // lanes, chunk, 0)

    @pl.when(step == steps - 1)
    def _():
        copy_hi.wait()
        copy_lo.wait()
        depth = 512
        f32 = jnp.float32
        for q in range(2):
            out_ref[q] = jnp.zeros(out_ref.shape[1:], f32)

            def kstep(kk, carry):
                k0 = pl.multiple_of(kk * depth, depth)
                cols = pl.ds(k0, depth)
                rows = lhs_ref.shape[2]
                both = lhs_ref[q, :, :, cols].reshape(2 * rows, depth)
                t_hi = th_ref[q, cols, :]
                t_lo = tl_ref[q, cols, :]
                acc = jnp.dot(both, t_hi, preferred_element_type=f32)
                acc = acc[:rows] + acc[rows:]
                acc = acc + jnp.dot(both[:rows], t_lo, preferred_element_type=f32)
                out_ref[q] += acc
                return carry

            lax.fori_loop(0, half // depth, kstep, 0)


def band_spectra(voltages, window, table, frames, first_slot, n_slots):
    in_dev, length = voltages.shape
    frame_len = window.shape[1]
    half = frame_len // 2
    band = table.shape[3]
    block = 16
    rows = n_slots * in_dev
    kernel = functools.partial(taps_dft_kernel, first_slot=first_slot, n_slots=n_slots)
    return pl.pallas_call(
        kernel,
        out_shape=jax.ShapeDtypeStruct((2, rows, band), jnp.float32),
        grid=(in_dev // block,),
        in_specs=[
            pl.BlockSpec((block, length), lambda g: (g, 0)),
            pl.BlockSpec((TAPS, frame_len), lambda g: (0, 0)),
            pl.BlockSpec(memory_space=pl.ANY),
        ],
        out_specs=pl.BlockSpec((2, rows, band), lambda g: (0, 0, 0)),
        scratch_shapes=[
            pltpu.VMEM((2, 2, rows, half), jnp.bfloat16),
            pltpu.VMEM((2, half, band), jnp.bfloat16),
            pltpu.VMEM((2, half, band), jnp.bfloat16),
            pltpu.SemaphoreType.DMA((2,)),
        ],
        compiler_params=pltpu.CompilerParams(vmem_limit_bytes=48 * 1024 * 1024),
    )(voltages, window, table)


def on_device(voltages, gains):
    in_dev, length = voltages.shape
    band = gains.shape[2]
    half_band = band // 2
    frame_len = 2 * CHANNELS
    frames = length // frame_len
    n_time = lax.axis_size("tm")
    n_station = lax.axis_size("stn")
    all_inputs = in_dev * n_station
    history = TAPS - 1
    window = jnp.asarray(window_table(CHANNELS))
    table = band_tables(frame_len, band)

    raw_next = band_spectra(voltages, window, table, frames, frames, history)
    given = passed_along(raw_next, "tm", 1)
    raw = band_spectra(voltages, window, table, frames, 0, frames)
    raw = raw.at[:, : history * in_dev, :].add(given)
    raw = jnp.transpose(raw, (0, 2, 1))

    row = frames * in_dev
    raw = jnp.transpose(raw.reshape(2, 2, half_band, row), (1, 2, 0, 3))
    raw_re, raw_im = raw[0], raw[1]
    g = jnp.transpose(gains.reshape(2, in_dev, half_band, 2), (0, 2, 3, 1))
    g = jnp.tile(g, (1, 1, 1, frames))
    gain_re, gain_im = g[0], g[1]
    spec_re = gain_re * raw_re - gain_im * raw_im
    spec_im = gain_re * raw_im + gain_im * raw_re
    spectra = jnp.stack([spec_re, spec_im], axis=2).astype(jnp.bfloat16)
    spectra = spectra.reshape(n_time * n_station, 2 * row)
    spectra = lax.all_to_all(spectra, ("tm", "stn"), split_axis=0, concat_axis=0, tiled=True)
    spectra = spectra.reshape(n_time, n_station, 2, frames, in_dev)
    stacked = jnp.transpose(spectra, (2, 0, 3, 1, 4)).reshape(2, n_time * frames, all_inputs)
    flipped = jnp.concatenate([stacked[1], -stacked[0]], axis=0)
    stacked = stacked.reshape(2 * n_time * frames, all_inputs)
    both = jnp.concatenate([stacked, flipped], axis=1)
    vis = jnp.einsum("ki,kj->ij", both, stacked, preferred_element_type=jnp.float32)
    vis = vis * (1.0 / float(n_time * frames))
    return vis.reshape(1, 2, all_inputs, all_inputs)


def solution(mesh):
    in_specs = (P("stn", "tm"), P(None, "stn", None))
    out_specs = P(("tm", "stn"), None, None, None)
    return jax.shard_map(
        on_device, mesh=mesh, in_specs=in_specs, out_specs=out_specs, check_vma=False
    )
```

```python
import functools

import numpy as np

import jax
import jax.numpy as jnp
from jax import lax
from jax.experimental import pallas as pl
from jax.experimental.pallas import tpu as pltpu
from jax.sharding import PartitionSpec as P

CHANNELS = 4096
BAND_LOW = 1024
TAPS = 8


def passed_along(x, axis, by):
    devices = lax.axis_size(axis)
    pairs = [(i, i + by) for i in range(devices) if 0 <= i + by < devices]
    return lax.ppermute(x, axis, pairs)


def window_table(chans):
    frame_len = 2 * chans
    total_len = TAPS * frame_len
    positions = np.arange(total_len, dtype=np.float64)
    centred = (positions - (total_len - 1) / 2.0) / frame_len
    taper = np.sin(np.pi * (positions + 0.5) / total_len)
    shaped = np.sinc(centred) * taper * taper
    shaped = shaped / np.sqrt(np.sum(shaped * shaped))
    return shaped.reshape(TAPS, frame_len).astype(np.float32)


def split(x):
    hi = lax.reduce_precision(x, exponent_bits=8, mantissa_bits=7)
    lo = x - hi
    return hi.astype(jnp.bfloat16), lo.astype(jnp.bfloat16)


def band_tables(frame_len, band):
    half = band // 2
    n_b = 32
    n_a = frame_len // 2 // n_b
    q = jnp.arange(2, dtype=jnp.int32)[:, None, None]
    k = jnp.arange(band, dtype=jnp.int32)[None, None, :]
    chan = 2 * (k % half) + q
    imag_col = k >= half
    a = jnp.arange(n_a, dtype=jnp.int32)[None, :, None]
    b = jnp.arange(n_b, dtype=jnp.int32)[None, :, None]
    p_steps = n_a * 2
    tp = (2.0 * jnp.pi / p_steps) * ((a * chan) % p_steps).astype(jnp.float32)
    tq = (2.0 * jnp.pi / frame_len) * ((b * (BAND_LOW + chan)) % frame_len).astype(jnp.float32)
    pr, pi = jnp.cos(tp), -jnp.sin(tp)
    qr, qi = jnp.cos(tq), -jnp.sin(tq)
    b1 = jnp.where(imag_col, qi, qr)
    b2 = jnp.where(imag_col, qr, -qi)
    t = pr[:, :, None, :] * b1[:, None, :, :] + pi[:, :, None, :] * b2[:, None, :, :]
    return t.reshape(2, n_a * n_b, band)


def taps_dft_kernel(x_ref, w_ref, table_hbm, out_ref, lhs_ref, table_ref, sem, *, first_slot, n_slots):
    step = pl.program_id(0)
    steps = pl.num_programs(0)
    block = x_ref.shape[0]
    inputs = block * steps
    frame_len = w_ref.shape[1]
    half = frame_len // 2
    frames = x_ref.shape[1] // frame_len
    history = TAPS - 1
    lanes = 128
    copy_table = pltpu.make_async_copy(table_hbm, table_ref, sem.at[0])

    @pl.when(step == 0)
    def _():
        copy_table.start()

    row0 = pl.multiple_of(step * block, block)

    def chunk(j, carry):
        base = pl.multiple_of(j * lanes, lanes)
        xs = []
        ws = []
        for offset in (0, half):
            xs.append([x_ref[:, pl.ds(f * frame_len + offset + base, lanes)].astype(jnp.float32) for f in range(frames)])
            ws.append([w_ref[pl.ds(p, 1), pl.ds(offset + base, lanes)] for p in range(TAPS)])
        for slot in range(n_slots):
            s = first_slot + slot
            accs = []
            for part in range(2):
                acc = None
                for p in range(TAPS):
                    g = s + p - history
                    if 0 <= g < frames:
                        term = ws[part][p] * xs[part][g]
                        acc = term if acc is None else acc + term
                accs.append(acc)
            folded = (accs[0] + accs[1], accs[0] - accs[1])
            rows = pl.ds(pl.multiple_of(slot * inputs + row0, block), block)
            for q in range(2):
                hi = folded[q].astype(jnp.bfloat16)
                lo = (folded[q] - hi.astype(jnp.float32)).astype(jnp.bfloat16)
                lhs_ref[q, 0, rows, pl.ds(base, lanes)] = hi
                lhs_ref[q, 1, rows, pl.ds(base, lanes)] = lo
        return carry

    lax.fori_loop(0, half // lanes, chunk, 0)

    @pl.when(step == steps - 1)
    def _():
        copy_table.wait()
        depth = 512
        f32 = jnp.float32
        for q in range(2):
            out_ref[q] = jnp.zeros(out_ref.shape[1:], f32)

            def kstep(kk, carry):
                k0 = pl.multiple_of(kk * depth, depth)
                cols = pl.ds(k0, depth)
                rows = lhs_ref.shape[2]
                both = lhs_ref[q, :, :, cols].reshape(2 * rows, depth)
                table = table_ref[q, cols, :]
                t_hi = table.astype(jnp.bfloat16)
                t_lo = (table - t_hi.astype(f32)).astype(jnp.bfloat16)
                acc = jnp.dot(both, t_hi, preferred_element_type=f32)
                acc = acc[:rows] + acc[rows:]
                acc = acc + jnp.dot(both[:rows], t_lo, preferred_element_type=f32)
                out_ref[q] += acc
                return carry

            lax.fori_loop(0, half // depth, kstep, 0)


def band_spectra(voltages, window, table, frames, first_slot, n_slots):
    in_dev, length = voltages.shape
    frame_len = window.shape[1]
    half = frame_len // 2
    band = table.shape[2]
    block = 16
    rows = n_slots * in_dev
    kernel = functools.partial(taps_dft_kernel, first_slot=first_slot, n_slots=n_slots)
    return pl.pallas_call(
        kernel,
        out_shape=jax.ShapeDtypeStruct((2, rows, band), jnp.float32),
        grid=(in_dev // block,),
        in_specs=[
            pl.BlockSpec((block, length), lambda g: (g, 0)),
            pl.BlockSpec((TAPS, frame_len), lambda g: (0, 0)),
            pl.BlockSpec(memory_space=pl.ANY),
        ],
        out_specs=pl.BlockSpec((2, rows, band), lambda g: (0, 0, 0)),
        scratch_shapes=[
            pltpu.VMEM((2, 2, rows, half), jnp.bfloat16),
            pltpu.VMEM((2, half, band), jnp.float32),
            pltpu.SemaphoreType.DMA((1,)),
        ],
        compiler_params=pltpu.CompilerParams(vmem_limit_bytes=48 * 1024 * 1024),
    )(voltages, window, table)


def on_device(voltages, gains):
    in_dev, length = voltages.shape
    band = gains.shape[2]
    half_band = band // 2
    frame_len = 2 * CHANNELS
    frames = length // frame_len
    n_time = lax.axis_size("tm")
    n_station = lax.axis_size("stn")
    all_inputs = in_dev * n_station
    history = TAPS - 1
    window = jnp.asarray(window_table(CHANNELS))
    table = band_tables(frame_len, band)

    raw_next = band_spectra(voltages, window, table, frames, frames, history)
    given = passed_along(raw_next, "tm", 1)
    raw = band_spectra(voltages, window, table, frames, 0, frames)
    raw = raw.at[:, : history * in_dev, :].add(given)
    raw = jnp.transpose(raw, (0, 2, 1))

    row = frames * in_dev
    raw = jnp.transpose(raw.reshape(2, 2, half_band, row), (1, 2, 0, 3))
    raw_re, raw_im = raw[0], raw[1]
    g = jnp.transpose(gains.reshape(2, in_dev, half_band, 2), (0, 2, 3, 1))
    g = jnp.tile(g, (1, 1, 1, frames))
    gain_re, gain_im = g[0], g[1]
    spec_re = gain_re * raw_re - gain_im * raw_im
    spec_im = gain_re * raw_im + gain_im * raw_re
    spectra = jnp.stack([spec_re, spec_im], axis=2).astype(jnp.bfloat16)
    spectra = spectra.reshape(n_time * n_station, 2 * row)
    spectra = lax.all_to_all(spectra, ("tm", "stn"), split_axis=0, concat_axis=0, tiled=True)
    spectra = spectra.reshape(n_time, n_station, 2, frames, in_dev)
    stacked = jnp.transpose(spectra, (2, 0, 3, 1, 4)).reshape(2, n_time * frames, all_inputs)
    flipped = jnp.concatenate([stacked[1], -stacked[0]], axis=0)
    stacked = stacked.reshape(2 * n_time * frames, all_inputs)
    both = jnp.concatenate([stacked, flipped], axis=1)
    vis = jnp.einsum("ki,kj->ij", both, stacked, preferred_element_type=jnp.float32)
    vis = vis * (1.0 / float(n_time * frames))
    return vis.reshape(1, 2, all_inputs, all_inputs)


def solution(mesh):
    in_specs = (P("stn", "tm"), P(None, "stn", None))
    out_specs = P(("tm", "stn"), None, None, None)
    return jax.shard_map(
        on_device, mesh=mesh, in_specs=in_specs, out_specs=out_specs, check_vma=False
    )
```

```python
import functools

import numpy as np

import jax
import jax.numpy as jnp
from jax import lax
from jax.experimental import pallas as pl
from jax.experimental.pallas import tpu as pltpu
from jax.sharding import PartitionSpec as P

CHANNELS = 4096
BAND_LOW = 1024
TAPS = 8


def passed_along(x, axis, by):
    devices = lax.axis_size(axis)
    pairs = [(i, i + by) for i in range(devices) if 0 <= i + by < devices]
    return lax.ppermute(x, axis, pairs)


def window_table(chans):
    frame_len = 2 * chans
    total_len = TAPS * frame_len
    positions = np.arange(total_len, dtype=np.float64)
    centred = (positions - (total_len - 1) / 2.0) / frame_len
    taper = np.sin(np.pi * (positions + 0.5) / total_len)
    shaped = np.sinc(centred) * taper * taper
    shaped = shaped / np.sqrt(np.sum(shaped * shaped))
    return shaped.reshape(TAPS, frame_len).astype(np.float32)


def split(x):
    hi = lax.reduce_precision(x, exponent_bits=8, mantissa_bits=7)
    lo = x - hi
    return hi.astype(jnp.bfloat16), lo.astype(jnp.bfloat16)


def band_tables(frame_len, band):
    half = band // 2
    n_b = 32
    n_a = frame_len // 2 // n_b
    q = jnp.arange(2, dtype=jnp.int32)[:, None, None]
    k = jnp.arange(band, dtype=jnp.int32)[None, None, :]
    chan = 2 * (k % half) + q
    imag_col = k >= half
    a = jnp.arange(n_a, dtype=jnp.int32)[None, :, None]
    b = jnp.arange(n_b, dtype=jnp.int32)[None, :, None]
    p_steps = n_a * 2
    tp = (2.0 * jnp.pi / p_steps) * ((a * chan) % p_steps).astype(jnp.float32)
    tq = (2.0 * jnp.pi / frame_len) * ((b * (BAND_LOW + chan)) % frame_len).astype(jnp.float32)
    pr, pi = jnp.cos(tp), -jnp.sin(tp)
    qr, qi = jnp.cos(tq), -jnp.sin(tq)
    b1 = jnp.where(imag_col, qi, qr)
    b2 = jnp.where(imag_col, qr, -qi)
    t = pr[:, :, None, :] * b1[:, None, :, :] + pi[:, :, None, :] * b2[:, None, :, :]
    return t.reshape(2, n_a * n_b, band)


def taps_dft_kernel(x_ref, w_ref, table_hbm, out_ref, lhs_ref, table_ref, sem, *, first_slot, n_slots):
    inputs = x_ref.shape[0]
    sub = 16
    frame_len = w_ref.shape[1]
    half = frame_len // 2
    frames = x_ref.shape[1] // frame_len
    history = TAPS - 1
    lanes = 128
    depth = 512
    spans = half // depth
    rows = lhs_ref.shape[2]
    f32 = jnp.float32
    copy_table = pltpu.make_async_copy(table_hbm, table_ref, sem.at[0])
    copy_table.start()

    def taps(base, row0):
        xs = []
        ws = []
        inputs_at = pl.ds(row0, sub)
        for offset in (0, half):
            xs.append([x_ref[inputs_at, pl.ds(f * frame_len + offset + base, lanes)].astype(f32) for f in range(frames)])
            ws.append([w_ref[pl.ds(p, 1), pl.ds(offset + base, lanes)] for p in range(TAPS)])
        for slot in range(n_slots):
            s = first_slot + slot
            accs = []
            for part in range(2):
                acc = None
                for p in range(TAPS):
                    g = s + p - history
                    if 0 <= g < frames:
                        term = ws[part][p] * xs[part][g]
                        acc = term if acc is None else acc + term
                accs.append(acc)
            folded = (accs[0] + accs[1], accs[0] - accs[1])
            at = pl.ds(slot * inputs + row0, sub)
            for q in range(2):
                hi = folded[q].astype(jnp.bfloat16)
                lo = (folded[q] - hi.astype(f32)).astype(jnp.bfloat16)
                lhs_ref[q, 0, at, pl.ds(base, lanes)] = hi
                lhs_ref[q, 1, at, pl.ds(base, lanes)] = lo

    def taps_span(kk):
        for c in range(depth // lanes):
            base = pl.multiple_of(kk * depth + c * lanes, lanes)
            for row0 in range(0, inputs, sub):
                taps(base, row0)

    def product(kk):
        k0 = pl.multiple_of(kk * depth, depth)
        cols = pl.ds(k0, depth)
        for q in range(2):
            both = lhs_ref[q, :, :, cols].reshape(2 * rows, depth)
            table = table_ref[q, cols, :]
            t_hi = table.astype(jnp.bfloat16)
            t_lo = (table - t_hi.astype(f32)).astype(jnp.bfloat16)
            acc = jnp.dot(both, t_hi, preferred_element_type=f32)
            acc = acc[:rows] + acc[rows:]
            acc = acc + jnp.dot(both[:rows], t_lo, preferred_element_type=f32)
            out_ref[q] += acc

    out_ref[...] = jnp.zeros(out_ref.shape, f32)
    taps_span(0)
    taps_span(1)
    copy_table.wait()
    product(0)

    def span(kk, carry):
        taps_span(kk)
        product(kk - 1)
        return carry

    lax.fori_loop(2, spans, span, 0)
    product(spans - 1)


def band_spectra(voltages, window, table, frames, first_slot, n_slots):
    in_dev, length = voltages.shape
    frame_len = window.shape[1]
    half = frame_len // 2
    band = table.shape[2]
    rows = n_slots * in_dev
    kernel = functools.partial(taps_dft_kernel, first_slot=first_slot, n_slots=n_slots)
    return pl.pallas_call(
        kernel,
        out_shape=jax.ShapeDtypeStruct((2, rows, band), jnp.float32),
        grid=(1,),
        in_specs=[
            pl.BlockSpec((in_dev, length), lambda g: (0, 0)),
            pl.BlockSpec((TAPS, frame_len), lambda g: (0, 0)),
            pl.BlockSpec(memory_space=pl.ANY),
        ],
        out_specs=pl.BlockSpec((2, rows, band), lambda g: (0, 0, 0)),
        scratch_shapes=[
            pltpu.VMEM((2, 2, rows, half), jnp.bfloat16),
            pltpu.VMEM((2, half, band), jnp.float32),
            pltpu.SemaphoreType.DMA((1,)),
        ],
        compiler_params=pltpu.CompilerParams(vmem_limit_bytes=56 * 1024 * 1024),
    )(voltages, window, table)


def on_device(voltages, gains):
    in_dev, length = voltages.shape
    band = gains.shape[2]
    half_band = band // 2
    frame_len = 2 * CHANNELS
    frames = length // frame_len
    n_time = lax.axis_size("tm")
    n_station = lax.axis_size("stn")
    all_inputs = in_dev * n_station
    history = TAPS - 1
    window = jnp.asarray(window_table(CHANNELS))
    table = band_tables(frame_len, band)

    raw_next = band_spectra(voltages, window, table, frames, frames, history)
    given = passed_along(raw_next, "tm", 1)
    raw = band_spectra(voltages, window, table, frames, 0, frames)
    raw = raw.at[:, : history * in_dev, :].add(given)
    raw = jnp.transpose(raw, (0, 2, 1))

    row = frames * in_dev
    raw = jnp.transpose(raw.reshape(2, 2, half_band, row), (1, 2, 0, 3))
    raw_re, raw_im = raw[0], raw[1]
    g = jnp.transpose(gains.reshape(2, in_dev, half_band, 2), (0, 2, 3, 1))
    g = jnp.tile(g, (1, 1, 1, frames))
    gain_re, gain_im = g[0], g[1]
    spec_re = gain_re * raw_re - gain_im * raw_im
    spec_im = gain_re * raw_im + gain_im * raw_re
    spectra = jnp.stack([spec_re, spec_im], axis=2).astype(jnp.bfloat16)
    spectra = spectra.reshape(n_time * n_station, 2 * row)
    spectra = lax.all_to_all(spectra, ("tm", "stn"), split_axis=0, concat_axis=0, tiled=True)
    spectra = spectra.reshape(n_time, n_station, 2, frames, in_dev)
    stacked = jnp.transpose(spectra, (2, 0, 3, 1, 4)).reshape(2, n_time * frames, all_inputs)
    flipped = jnp.concatenate([stacked[1], -stacked[0]], axis=0)
    stacked = stacked.reshape(2 * n_time * frames, all_inputs)
    both = jnp.concatenate([stacked, flipped], axis=1)
    vis = jnp.einsum("ki,kj->ij", both, stacked, preferred_element_type=jnp.float32)
    vis = vis * (1.0 / float(n_time * frames))
    return vis.reshape(1, 2, all_inputs, all_inputs)


def solution(mesh):
    in_specs = (P("stn", "tm"), P(None, "stn", None))
    out_specs = P(("tm", "stn"), None, None, None)
    return jax.shard_map(
        on_device, mesh=mesh, in_specs=in_specs, out_specs=out_specs, check_vma=False
    )
```

```python
import functools

import numpy as np

import jax
import jax.numpy as jnp
from jax import lax
from jax.experimental import pallas as pl
from jax.experimental.pallas import tpu as pltpu
from jax.sharding import PartitionSpec as P

CHANNELS = 4096
BAND_LOW = 1024
TAPS = 8


def passed_along(x, axis, by):
    devices = lax.axis_size(axis)
    pairs = [(i, i + by) for i in range(devices) if 0 <= i + by < devices]
    return lax.ppermute(x, axis, pairs)


def window_table(chans):
    frame_len = 2 * chans
    total_len = TAPS * frame_len
    positions = np.arange(total_len, dtype=np.float64)
    centred = (positions - (total_len - 1) / 2.0) / frame_len
    taper = np.sin(np.pi * (positions + 0.5) / total_len)
    shaped = np.sinc(centred) * taper * taper
    shaped = shaped / np.sqrt(np.sum(shaped * shaped))
    return shaped.reshape(TAPS, frame_len).astype(np.float32)


def split(x):
    hi = lax.reduce_precision(x, exponent_bits=8, mantissa_bits=7)
    lo = x - hi
    return hi.astype(jnp.bfloat16), lo.astype(jnp.bfloat16)


def band_tables(frame_len, band):
    half = band // 2
    n_b = 32
    n_a = frame_len // 2 // n_b
    q = jnp.arange(2, dtype=jnp.int32)[:, None, None]
    k = jnp.arange(band, dtype=jnp.int32)[None, None, :]
    chan = 2 * (k % half) + q
    imag_col = k >= half
    a = jnp.arange(n_a, dtype=jnp.int32)[None, :, None]
    b = jnp.arange(n_b, dtype=jnp.int32)[None, :, None]
    p_steps = n_a * 2
    tp = (2.0 * jnp.pi / p_steps) * ((a * chan) % p_steps).astype(jnp.float32)
    tq = (2.0 * jnp.pi / frame_len) * ((b * (BAND_LOW + chan)) % frame_len).astype(jnp.float32)
    pr, pi = jnp.cos(tp), -jnp.sin(tp)
    qr, qi = jnp.cos(tq), -jnp.sin(tq)
    b1 = jnp.where(imag_col, qi, qr)
    b2 = jnp.where(imag_col, qr, -qi)
    t = pr[:, :, None, :] * b1[:, None, :, :] + pi[:, :, None, :] * b2[:, None, :, :]
    return t.reshape(2, n_a * n_b, band)


def taps_dft_kernel(x_ref, w_ref, table_hbm, out_ref, lhs_ref, table_ref, sem, *, first_slot, n_slots):
    step = pl.program_id(0)
    steps = pl.num_programs(0)
    block = x_ref.shape[0]
    inputs = block * steps
    frame_len = w_ref.shape[1]
    half = frame_len // 2
    frames = x_ref.shape[1] // frame_len
    history = TAPS - 1
    lanes = 128
    copy_table = pltpu.make_async_copy(table_hbm, table_ref, sem.at[0])

    @pl.when(step == 0)
    def _():
        copy_table.start()

    row0 = pl.multiple_of(step * block, block)

    def chunk(j, carry):
        base = pl.multiple_of(j * lanes, lanes)
        xs = []
        ws = []
        for offset in (0, half):
            xs.append([x_ref[:, pl.ds(f * frame_len + offset + base, lanes)].astype(jnp.float32) for f in range(frames)])
            ws.append([w_ref[pl.ds(p, 1), pl.ds(offset + base, lanes)] for p in range(TAPS)])
        for slot in range(n_slots):
            s = first_slot + slot
            accs = []
            for part in range(2):
                acc = None
                for p in range(TAPS):
                    g = s + p - history
                    if 0 <= g < frames:
                        term = ws[part][p] * xs[part][g]
                        acc = term if acc is None else acc + term
                accs.append(acc)
            folded = (accs[0] + accs[1], accs[0] - accs[1])
            rows = pl.ds(pl.multiple_of(slot * inputs + row0, block), block)
            for q in range(2):
                hi = folded[q].astype(jnp.bfloat16)
                lo = (folded[q] - hi.astype(jnp.float32)).astype(jnp.bfloat16)
                lhs_ref[q, 0, rows, pl.ds(base, lanes)] = hi
                lhs_ref[q, 1, rows, pl.ds(base, lanes)] = lo
        return carry

    lax.fori_loop(0, half // lanes, chunk, 0)

    @pl.when(step == steps - 1)
    def _():
        copy_table.wait()
        depth = 512
        f32 = jnp.float32
        for q in range(2):
            out_ref[q] = jnp.zeros(out_ref.shape[1:], f32)

            def kstep(kk, carry):
                k0 = pl.multiple_of(kk * depth, depth)
                cols = pl.ds(k0, depth)
                rows = lhs_ref.shape[2]
                both = lhs_ref[q, :, :, cols].reshape(2 * rows, depth)
                table = table_ref[q, cols, :]
                t_hi = table.astype(jnp.bfloat16)
                t_lo = (table - t_hi.astype(f32)).astype(jnp.bfloat16)
                acc = jnp.dot(both, t_hi, preferred_element_type=f32)
                acc = acc[:rows] + acc[rows:]
                acc = acc + jnp.dot(both[:rows], t_lo, preferred_element_type=f32)
                out_ref[q] += acc
                return carry

            lax.fori_loop(0, half // depth, kstep, 0)


def band_spectra(voltages, window, table, frames, first_slot, n_slots):
    in_dev, length = voltages.shape
    frame_len = window.shape[1]
    half = frame_len // 2
    band = table.shape[2]
    block = 16
    rows = n_slots * in_dev
    kernel = functools.partial(taps_dft_kernel, first_slot=first_slot, n_slots=n_slots)
    return pl.pallas_call(
        kernel,
        out_shape=jax.ShapeDtypeStruct((2, rows, band), jnp.float32),
        grid=(in_dev // block,),
        in_specs=[
            pl.BlockSpec((block, length), lambda g: (g, 0)),
            pl.BlockSpec((TAPS, frame_len), lambda g: (0, 0)),
            pl.BlockSpec(memory_space=pl.ANY),
        ],
        out_specs=pl.BlockSpec((2, rows, band), lambda g: (0, 0, 0)),
        scratch_shapes=[
            pltpu.VMEM((2, 2, rows, half), jnp.bfloat16),
            pltpu.VMEM((2, half, band), jnp.float32),
            pltpu.SemaphoreType.DMA((1,)),
        ],
        compiler_params=pltpu.CompilerParams(vmem_limit_bytes=48 * 1024 * 1024),
    )(voltages, window, table)


def cross_kernel(lhs_ref, rhs_ref, out_ref, *, scale):
    nt = (((1,), (1,)), ((), ()))
    out = lax.dot_general(lhs_ref[...], rhs_ref[...], nt, preferred_element_type=jnp.float32)
    out_ref[...] = out * scale


def cross_power(both, stacked, scale):
    rows, depth = both.shape
    cols = stacked.shape[0]
    block = 256
    return pl.pallas_call(
        functools.partial(cross_kernel, scale=scale),
        out_shape=jax.ShapeDtypeStruct((rows, cols), jnp.float32),
        grid=(rows // block,),
        in_specs=[
            pl.BlockSpec((block, depth), lambda g: (g, 0)),
            pl.BlockSpec((cols, depth), lambda g: (0, 0)),
        ],
        out_specs=pl.BlockSpec((block, cols), lambda g: (g, 0)),
    )(both, stacked)


def on_device(voltages, gains):
    in_dev, length = voltages.shape
    band = gains.shape[2]
    half_band = band // 2
    frame_len = 2 * CHANNELS
    frames = length // frame_len
    n_time = lax.axis_size("tm")
    n_station = lax.axis_size("stn")
    all_inputs = in_dev * n_station
    history = TAPS - 1
    window = jnp.asarray(window_table(CHANNELS))
    table = band_tables(frame_len, band)

    raw_next = band_spectra(voltages, window, table, frames, frames, history)
    given = passed_along(raw_next, "tm", 1)
    raw = band_spectra(voltages, window, table, frames, 0, frames)
    raw = raw.at[:, : history * in_dev, :].add(given)
    raw = jnp.transpose(raw, (0, 2, 1))

    row = frames * in_dev
    raw = jnp.transpose(raw.reshape(2, 2, half_band, row), (1, 2, 0, 3))
    raw_re, raw_im = raw[0], raw[1]
    g = jnp.transpose(gains.reshape(2, in_dev, half_band, 2), (0, 2, 3, 1))
    g = jnp.tile(g, (1, 1, 1, frames))
    gain_re, gain_im = g[0], g[1]
    spec_re = gain_re * raw_re - gain_im * raw_im
    spec_im = gain_re * raw_im + gain_im * raw_re
    spectra = jnp.stack([spec_re, spec_im], axis=2).astype(jnp.bfloat16)
    spectra = spectra.reshape(n_time * n_station, 2 * row)
    spectra = lax.all_to_all(spectra, ("tm", "stn"), split_axis=0, concat_axis=0, tiled=True)
    spectra = spectra.reshape(n_time, n_station, 2, frames, in_dev)
    stacked = jnp.transpose(spectra, (1, 4, 2, 0, 3)).reshape(all_inputs, 2, n_time * frames)
    flipped = jnp.concatenate([stacked[:, 1], -stacked[:, 0]], axis=1)
    stacked = stacked.reshape(all_inputs, 2 * n_time * frames)
    both = jnp.concatenate([stacked, flipped], axis=0)
    vis = cross_power(both, stacked, 1.0 / float(n_time * frames))
    return vis.reshape(1, 2, all_inputs, all_inputs)


def solution(mesh):
    in_specs = (P("stn", "tm"), P(None, "stn", None))
    out_specs = P(("tm", "stn"), None, None, None)
    return jax.shard_map(
        on_device, mesh=mesh, in_specs=in_specs, out_specs=out_specs, check_vma=False
    )
```

```python
import functools

import numpy as np

import jax
import jax.numpy as jnp
from jax import lax
from jax.experimental import pallas as pl
from jax.experimental.pallas import tpu as pltpu
from jax.sharding import PartitionSpec as P

CHANNELS = 4096
BAND_LOW = 1024
TAPS = 8


def passed_along(x, axis, by):
    devices = lax.axis_size(axis)
    pairs = [(i, i + by) for i in range(devices) if 0 <= i + by < devices]
    return lax.ppermute(x, axis, pairs)


def window_table(chans):
    frame_len = 2 * chans
    total_len = TAPS * frame_len
    positions = np.arange(total_len, dtype=np.float64)
    centred = (positions - (total_len - 1) / 2.0) / frame_len
    taper = np.sin(np.pi * (positions + 0.5) / total_len)
    shaped = np.sinc(centred) * taper * taper
    shaped = shaped / np.sqrt(np.sum(shaped * shaped))
    return shaped.reshape(TAPS, frame_len).astype(np.float32)


def split(x):
    hi = lax.reduce_precision(x, exponent_bits=8, mantissa_bits=7)
    lo = x - hi
    return hi.astype(jnp.bfloat16), lo.astype(jnp.bfloat16)


def band_tables(frame_len, band):
    half = band // 2
    n_b = 32
    n_a = frame_len // 2 // n_b
    q = jnp.arange(2, dtype=jnp.int32)[:, None, None]
    k = jnp.arange(band, dtype=jnp.int32)[None, None, :]
    chan = 2 * (k % half) + q
    imag_col = k >= half
    a = jnp.arange(n_a, dtype=jnp.int32)[None, :, None]
    b = jnp.arange(n_b, dtype=jnp.int32)[None, :, None]
    p_steps = n_a * 2
    tp = (2.0 * jnp.pi / p_steps) * ((a * chan) % p_steps).astype(jnp.float32)
    tq = (2.0 * jnp.pi / frame_len) * ((b * (BAND_LOW + chan)) % frame_len).astype(jnp.float32)
    pr, pi = jnp.cos(tp), -jnp.sin(tp)
    qr, qi = jnp.cos(tq), -jnp.sin(tq)
    b1 = jnp.where(imag_col, qi, qr)
    b2 = jnp.where(imag_col, qr, -qi)
    return table_product(pr, pi, b1, b2)


def table_kernel(pr_ref, pi_ref, b1_ref, b2_ref, out_ref):
    n_b = b1_ref.shape[1]
    b1 = b1_ref[0]
    b2 = b2_ref[0]
    for a in range(pr_ref.shape[1]):
        at = pl.ds(a, 1)
        out_ref[0, pl.ds(a * n_b, n_b), :] = pr_ref[0, at, :] * b1 + pi_ref[0, at, :] * b2


def table_product(pr, pi, b1, b2):
    parts, n_a, band = pr.shape
    n_b = b1.shape[1]
    block = 16
    return pl.pallas_call(
        table_kernel,
        out_shape=jax.ShapeDtypeStruct((parts, n_a * n_b, band), jnp.float32),
        grid=(parts, n_a // block),
        in_specs=[
            pl.BlockSpec((1, block, band), lambda q, g: (q, g, 0)),
            pl.BlockSpec((1, block, band), lambda q, g: (q, g, 0)),
            pl.BlockSpec((1, n_b, band), lambda q, g: (q, 0, 0)),
            pl.BlockSpec((1, n_b, band), lambda q, g: (q, 0, 0)),
        ],
        out_specs=pl.BlockSpec((1, block * n_b, band), lambda q, g: (q, g, 0)),
    )(pr, pi, b1, b2)


def taps_dft_kernel(x_ref, w_ref, table_hbm, out_ref, lhs_ref, table_ref, sem, *, first_slot, n_slots):
    step = pl.program_id(0)
    steps = pl.num_programs(0)
    block = x_ref.shape[0]
    inputs = block * steps
    frame_len = w_ref.shape[1]
    half = frame_len // 2
    frames = x_ref.shape[1] // frame_len
    history = TAPS - 1
    lanes = 128
    copy_table = pltpu.make_async_copy(table_hbm, table_ref, sem.at[0])

    @pl.when(step == 0)
    def _():
        copy_table.start()

    row0 = pl.multiple_of(step * block, block)

    def chunk(j, carry):
        base = pl.multiple_of(j * lanes, lanes)
        for r0 in range(0, block, 8):
            inputs_at = pl.ds(r0, 8)
            xs = []
            ws = []
            for offset in (0, half):
                xs.append([x_ref[inputs_at, pl.ds(f * frame_len + offset + base, lanes)].astype(jnp.float32) for f in range(frames)])
                ws.append([w_ref[pl.ds(p, 1), pl.ds(offset + base, lanes)] for p in range(TAPS)])
            for slot in range(n_slots):
                s = first_slot + slot
                accs = []
                for part in range(2):
                    acc = None
                    for p in range(TAPS):
                        g = s + p - history
                        if 0 <= g < frames:
                            term = ws[part][p] * xs[part][g]
                            acc = term if acc is None else acc + term
                    accs.append(acc)
                folded = (accs[0] + accs[1], accs[0] - accs[1])
                rows = pl.ds(pl.multiple_of(slot * inputs + row0 + r0, 8), 8)
                for q in range(2):
                    hi = folded[q].astype(jnp.bfloat16)
                    lo = (folded[q] - hi.astype(jnp.float32)).astype(jnp.bfloat16)
                    lhs_ref[q, 0, rows, pl.ds(base, lanes)] = hi
                    lhs_ref[q, 1, rows, pl.ds(base, lanes)] = lo
        return carry

    lax.fori_loop(0, half // lanes, chunk, 0)

    @pl.when(step == steps - 1)
    def _():
        copy_table.wait()
        depth = 512
        f32 = jnp.float32
        for q in range(2):
            out_ref[q] = jnp.zeros(out_ref.shape[1:], f32)

            def kstep(kk, carry):
                k0 = pl.multiple_of(kk * depth, depth)
                cols = pl.ds(k0, depth)
                rows = lhs_ref.shape[2]
                both = lhs_ref[q, :, :, cols].reshape(2 * rows, depth)
                table = table_ref[q, cols, :]
                t_hi = table.astype(jnp.bfloat16)
                t_lo = (table - t_hi.astype(f32)).astype(jnp.bfloat16)
                acc = jnp.dot(both, t_hi, preferred_element_type=f32)
                acc = acc[:rows] + acc[rows:]
                acc = acc + jnp.dot(both[:rows], t_lo, preferred_element_type=f32)
                out_ref[q] += acc
                return carry

            lax.fori_loop(0, half // depth, kstep, 0)


def band_spectra(voltages, window, table, frames, first_slot, n_slots):
    in_dev, length = voltages.shape
    frame_len = window.shape[1]
    half = frame_len // 2
    band = table.shape[2]
    block = 16
    rows = n_slots * in_dev
    kernel = functools.partial(taps_dft_kernel, first_slot=first_slot, n_slots=n_slots)
    return pl.pallas_call(
        kernel,
        out_shape=jax.ShapeDtypeStruct((2, rows, band), jnp.float32),
        grid=(in_dev // block,),
        in_specs=[
            pl.BlockSpec((block, length), lambda g: (g, 0)),
            pl.BlockSpec((TAPS, frame_len), lambda g: (0, 0)),
            pl.BlockSpec(memory_space=pl.ANY),
        ],
        out_specs=pl.BlockSpec((2, rows, band), lambda g: (0, 0, 0)),
        scratch_shapes=[
            pltpu.VMEM((2, 2, rows, half), jnp.bfloat16),
            pltpu.VMEM((2, half, band), jnp.float32),
            pltpu.SemaphoreType.DMA((1,)),
        ],
        compiler_params=pltpu.CompilerParams(vmem_limit_bytes=48 * 1024 * 1024),
    )(voltages, window, table)


def on_device(voltages, gains):
    in_dev, length = voltages.shape
    band = gains.shape[2]
    half_band = band // 2
    frame_len = 2 * CHANNELS
    frames = length // frame_len
    n_time = lax.axis_size("tm")
    n_station = lax.axis_size("stn")
    all_inputs = in_dev * n_station
    history = TAPS - 1
    window = jnp.asarray(window_table(CHANNELS))
    table = band_tables(frame_len, band)

    raw_next = band_spectra(voltages, window, table, frames, frames, history)
    given = passed_along(raw_next, "tm", 1)
    raw = band_spectra(voltages, window, table, frames, 0, frames)
    raw = raw.at[:, : history * in_dev, :].add(given)
    raw = jnp.transpose(raw, (0, 2, 1))

    row = frames * in_dev
    raw = jnp.transpose(raw.reshape(2, 2, half_band, row), (1, 2, 0, 3))
    raw_re, raw_im = raw[0], raw[1]
    g = jnp.transpose(gains.reshape(2, in_dev, half_band, 2), (0, 2, 3, 1))
    g = jnp.tile(g, (1, 1, 1, frames))
    gain_re, gain_im = g[0], g[1]
    spec_re = gain_re * raw_re - gain_im * raw_im
    spec_im = gain_re * raw_im + gain_im * raw_re
    spectra = jnp.stack([spec_re, spec_im], axis=2).astype(jnp.bfloat16)
    spectra = spectra.reshape(n_time * n_station, 2 * row)
    spectra = lax.all_to_all(spectra, ("tm", "stn"), split_axis=0, concat_axis=0, tiled=True)
    spectra = spectra.reshape(n_time, n_station, 2, frames, in_dev)
    stacked = jnp.transpose(spectra, (2, 0, 3, 1, 4)).reshape(2, n_time * frames, all_inputs)
    flipped = jnp.concatenate([stacked[1], -stacked[0]], axis=0)
    stacked = stacked.reshape(2 * n_time * frames, all_inputs)
    both = jnp.concatenate([stacked, flipped], axis=1)
    vis = jnp.einsum("ki,kj->ij", both, stacked, preferred_element_type=jnp.float32)
    vis = vis * (1.0 / float(n_time * frames))
    return vis.reshape(1, 2, all_inputs, all_inputs)


def solution(mesh):
    in_specs = (P("stn", "tm"), P(None, "stn", None))
    out_specs = P(("tm", "stn"), None, None, None)
    return jax.shard_map(
        on_device, mesh=mesh, in_specs=in_specs, out_specs=out_specs, check_vma=False
    )
```

```python
import functools

import numpy as np

import jax
import jax.numpy as jnp
from jax import lax
from jax.experimental import pallas as pl
from jax.experimental.pallas import tpu as pltpu
from jax.sharding import PartitionSpec as P

CHANNELS = 4096
BAND_LOW = 1024
TAPS = 8


def passed_along(x, axis, by):
    devices = lax.axis_size(axis)
    pairs = [(i, i + by) for i in range(devices) if 0 <= i + by < devices]
    return lax.ppermute(x, axis, pairs)


def window_table(chans):
    frame_len = 2 * chans
    total_len = TAPS * frame_len
    positions = np.arange(total_len, dtype=np.float64)
    centred = (positions - (total_len - 1) / 2.0) / frame_len
    taper = np.sin(np.pi * (positions + 0.5) / total_len)
    shaped = np.sinc(centred) * taper * taper
    shaped = shaped / np.sqrt(np.sum(shaped * shaped))
    return shaped.reshape(TAPS, frame_len).astype(np.float32)


def split(x):
    hi = lax.reduce_precision(x, exponent_bits=8, mantissa_bits=7)
    lo = x - hi
    return hi.astype(jnp.bfloat16), lo.astype(jnp.bfloat16)


def band_tables(frame_len, band):
    half = band // 2
    n_b = 32
    n_a = frame_len // 2 // n_b
    q = jnp.arange(2, dtype=jnp.int32)[:, None, None]
    k = jnp.arange(band, dtype=jnp.int32)[None, None, :]
    chan = 2 * (k % half) + q
    imag_col = k >= half
    a = jnp.arange(n_a, dtype=jnp.int32)[None, :, None]
    b = jnp.arange(n_b, dtype=jnp.int32)[None, :, None]
    p_steps = n_a * 2
    tp = (2.0 * jnp.pi / p_steps) * ((a * chan) % p_steps).astype(jnp.float32)
    tq = (2.0 * jnp.pi / frame_len) * ((b * (BAND_LOW + chan)) % frame_len).astype(jnp.float32)
    pr, pi = jnp.cos(tp), -jnp.sin(tp)
    qr, qi = jnp.cos(tq), -jnp.sin(tq)
    b1 = jnp.where(imag_col, qi, qr)
    b2 = jnp.where(imag_col, qr, -qi)
    t = pr[:, :, None, :] * b1[:, None, :, :] + pi[:, :, None, :] * b2[:, None, :, :]
    return t.reshape(2, n_a * n_b, band)


def taps_dft_kernel(x_ref, w_ref, table_hbm, out_ref, lhs_ref, table_ref, sem, *, first_slot, n_slots):
    step = pl.program_id(0)
    steps = pl.num_programs(0)
    block = x_ref.shape[0]
    inputs = block * steps
    frame_len = w_ref.shape[1]
    half = frame_len // 2
    frames = x_ref.shape[1] // frame_len
    history = TAPS - 1
    lanes = 128
    copy_table = pltpu.make_async_copy(table_hbm, table_ref, sem.at[0])

    @pl.when(step == 0)
    def _():
        copy_table.start()

    row0 = pl.multiple_of(step * block, block)

    def chunk(j, carry):
        base = pl.multiple_of(j * lanes, lanes)
        for r0 in range(0, block, 8):
            inputs_at = pl.ds(r0, 8)
            xs = []
            ws = []
            for offset in (0, half):
                xs.append([x_ref[inputs_at, pl.ds(f * frame_len + offset + base, lanes)].astype(jnp.float32) for f in range(frames)])
                ws.append([w_ref[pl.ds(p, 1), pl.ds(offset + base, lanes)] for p in range(TAPS)])
            for slot in range(n_slots):
                s = first_slot + slot
                accs = []
                for part in range(2):
                    acc = None
                    for p in range(TAPS):
                        g = s + p - history
                        if 0 <= g < frames:
                            term = ws[part][p] * xs[part][g]
                            acc = term if acc is None else acc + term
                    accs.append(acc)
                folded = (accs[0] + accs[1], accs[0] - accs[1])
                rows = pl.ds(pl.multiple_of(slot * inputs + row0 + r0, 8), 8)
                for q in range(2):
                    lhs_ref[q, rows, pl.ds(base, lanes)] = folded[q]
        return carry

    lax.fori_loop(0, half // lanes, chunk, 0)

    @pl.when(step == steps - 1)
    def _():
        copy_table.wait()
        depth = 512
        f32 = jnp.float32
        for q in range(2):
            out_ref[q] = jnp.zeros(out_ref.shape[1:], f32)

            def kstep(kk, carry):
                k0 = pl.multiple_of(kk * depth, depth)
                cols = pl.ds(k0, depth)
                folded = lhs_ref[q, :, cols]
                l_hi = folded.astype(jnp.bfloat16)
                l_lo = (folded - l_hi.astype(f32)).astype(jnp.bfloat16)
                table = table_ref[q, cols, :]
                t_hi = table.astype(jnp.bfloat16)
                t_lo = (table - t_hi.astype(f32)).astype(jnp.bfloat16)
                acc = jnp.dot(l_hi, t_hi, preferred_element_type=f32)
                acc = acc + jnp.dot(l_lo, t_hi, preferred_element_type=f32)
                acc = acc + jnp.dot(l_hi, t_lo, preferred_element_type=f32)
                out_ref[q] += acc
                return carry

            lax.fori_loop(0, half // depth, kstep, 0)


def band_spectra(voltages, window, table, frames, first_slot, n_slots):
    in_dev, length = voltages.shape
    frame_len = window.shape[1]
    half = frame_len // 2
    band = table.shape[2]
    block = 16
    rows = n_slots * in_dev
    kernel = functools.partial(taps_dft_kernel, first_slot=first_slot, n_slots=n_slots)
    return pl.pallas_call(
        kernel,
        out_shape=jax.ShapeDtypeStruct((2, rows, band), jnp.float32),
        grid=(in_dev // block,),
        in_specs=[
            pl.BlockSpec((block, length), lambda g: (g, 0)),
            pl.BlockSpec((TAPS, frame_len), lambda g: (0, 0)),
            pl.BlockSpec(memory_space=pl.ANY),
        ],
        out_specs=pl.BlockSpec((2, rows, band), lambda g: (0, 0, 0)),
        scratch_shapes=[
            pltpu.VMEM((2, rows, half), jnp.float32),
            pltpu.VMEM((2, half, band), jnp.float32),
            pltpu.SemaphoreType.DMA((1,)),
        ],
        compiler_params=pltpu.CompilerParams(vmem_limit_bytes=48 * 1024 * 1024),
    )(voltages, window, table)


def on_device(voltages, gains):
    in_dev, length = voltages.shape
    band = gains.shape[2]
    half_band = band // 2
    frame_len = 2 * CHANNELS
    frames = length // frame_len
    n_time = lax.axis_size("tm")
    n_station = lax.axis_size("stn")
    all_inputs = in_dev * n_station
    history = TAPS - 1
    window = jnp.asarray(window_table(CHANNELS))
    table = band_tables(frame_len, band)

    raw_next = band_spectra(voltages, window, table, frames, frames, history)
    given = passed_along(raw_next, "tm", 1)
    raw = band_spectra(voltages, window, table, frames, 0, frames)
    raw = raw.at[:, : history * in_dev, :].add(given)
    raw = jnp.transpose(raw, (0, 2, 1))

    row = frames * in_dev
    raw = jnp.transpose(raw.reshape(2, 2, half_band, row), (1, 2, 0, 3))
    raw_re, raw_im = raw[0], raw[1]
    g = jnp.transpose(gains.reshape(2, in_dev, half_band, 2), (0, 2, 3, 1))
    g = jnp.tile(g, (1, 1, 1, frames))
    gain_re, gain_im = g[0], g[1]
    spec_re = gain_re * raw_re - gain_im * raw_im
    spec_im = gain_re * raw_im + gain_im * raw_re
    spectra = jnp.stack([spec_re, spec_im], axis=2).astype(jnp.bfloat16)
    spectra = spectra.reshape(n_time * n_station, 2 * row)
    spectra = lax.all_to_all(spectra, ("tm", "stn"), split_axis=0, concat_axis=0, tiled=True)
    spectra = spectra.reshape(n_time, n_station, 2, frames, in_dev)
    stacked = jnp.transpose(spectra, (2, 0, 3, 1, 4)).reshape(2, n_time * frames, all_inputs)
    flipped = jnp.concatenate([stacked[1], -stacked[0]], axis=0)
    stacked = stacked.reshape(2 * n_time * frames, all_inputs)
    both = jnp.concatenate([stacked, flipped], axis=1)
    vis = jnp.einsum("ki,kj->ij", both, stacked, preferred_element_type=jnp.float32)
    vis = vis * (1.0 / float(n_time * frames))
    return vis.reshape(1, 2, all_inputs, all_inputs)


def solution(mesh):
    in_specs = (P("stn", "tm"), P(None, "stn", None))
    out_specs = P(("tm", "stn"), None, None, None)
    return jax.shard_map(
        on_device, mesh=mesh, in_specs=in_specs, out_specs=out_specs, check_vma=False
    )
```

```python
import functools

import numpy as np

import jax
import jax.numpy as jnp
from jax import lax
from jax.experimental import pallas as pl
from jax.experimental.pallas import tpu as pltpu
from jax.sharding import PartitionSpec as P

CHANNELS = 4096
BAND_LOW = 1024
TAPS = 8


def passed_along(x, axis, by):
    devices = lax.axis_size(axis)
    pairs = [(i, i + by) for i in range(devices) if 0 <= i + by < devices]
    return lax.ppermute(x, axis, pairs)


def window_table(chans):
    frame_len = 2 * chans
    total_len = TAPS * frame_len
    positions = np.arange(total_len, dtype=np.float64)
    centred = (positions - (total_len - 1) / 2.0) / frame_len
    taper = np.sin(np.pi * (positions + 0.5) / total_len)
    shaped = np.sinc(centred) * taper * taper
    shaped = shaped / np.sqrt(np.sum(shaped * shaped))
    return shaped.reshape(TAPS, frame_len).astype(np.float32)


def split(x):
    hi = lax.reduce_precision(x, exponent_bits=8, mantissa_bits=7)
    lo = x - hi
    return hi.astype(jnp.bfloat16), lo.astype(jnp.bfloat16)


def band_tables(frame_len, band):
    half = band // 2
    n_b = 32
    n_a = frame_len // 2 // n_b
    q = jnp.arange(2, dtype=jnp.int32)[:, None, None]
    k = jnp.arange(band, dtype=jnp.int32)[None, None, :]
    chan = 2 * (k % half) + q
    imag_col = k >= half
    a = jnp.arange(n_a, dtype=jnp.int32)[None, :, None]
    b = jnp.arange(n_b, dtype=jnp.int32)[None, :, None]
    p_steps = n_a * 2
    tp = (2.0 * jnp.pi / p_steps) * ((a * chan) % p_steps).astype(jnp.float32)
    tq = (2.0 * jnp.pi / frame_len) * ((b * (BAND_LOW + chan)) % frame_len).astype(jnp.float32)
    pr, pi = jnp.cos(tp), -jnp.sin(tp)
    qr, qi = jnp.cos(tq), -jnp.sin(tq)
    b1 = jnp.where(imag_col, qi, qr)
    b2 = jnp.where(imag_col, qr, -qi)
    t = pr[:, :, None, :] * b1[:, None, :, :] + pi[:, :, None, :] * b2[:, None, :, :]
    return t.reshape(2, n_a * n_b, band)


def taps_dft_kernel(x_ref, w_ref, table_hbm, out_ref, lhs_ref, table_ref, sem, *, first_slot, n_slots):
    step = pl.program_id(0)
    steps = pl.num_programs(0)
    block = x_ref.shape[0]
    inputs = block * steps
    frame_len = w_ref.shape[1]
    half = frame_len // 2
    frames = x_ref.shape[1] // frame_len
    history = TAPS - 1
    lanes = 128
    copy_table = pltpu.make_async_copy(table_hbm, table_ref, sem.at[0])

    @pl.when(step == 0)
    def _():
        copy_table.start()

    row0 = pl.multiple_of(step * block, block)

    def chunk(j, carry):
        base = pl.multiple_of(j * lanes, lanes)
        for r0 in range(0, block, 8):
            inputs_at = pl.ds(r0, 8)
            xs = []
            ws = []
            for offset in (0, half):
                xs.append([x_ref[inputs_at, pl.ds(f * frame_len + offset + base, lanes)].astype(jnp.float32) for f in range(frames)])
                ws.append([w_ref[pl.ds(p, 1), pl.ds(offset + base, lanes)] for p in range(TAPS)])
            for slot in range(n_slots):
                s = first_slot + slot
                accs = []
                for part in range(2):
                    acc = None
                    for p in range(TAPS):
                        g = s + p - history
                        if 0 <= g < frames:
                            term = ws[part][p] * xs[part][g]
                            acc = term if acc is None else acc + term
                    accs.append(acc)
                rows = pl.ds(pl.multiple_of(slot * inputs + row0 + r0, 8), 8)
                lhs_ref[rows, pl.ds(base, lanes)] = accs[0]
                lhs_ref[rows, pl.ds(half + base, lanes)] = accs[1]
        return carry

    lax.fori_loop(0, half // lanes, chunk, 0)

    @pl.when(step == steps - 1)
    def _():
        copy_table.wait()
        depth = 512
        f32 = jnp.float32
        out_ref[...] = jnp.zeros(out_ref.shape, f32)

        def kstep(kk, carry):
            k0 = pl.multiple_of(kk * depth, depth)
            cols = pl.ds(k0, depth)
            first = lhs_ref[:, cols]
            second = lhs_ref[:, pl.ds(half + k0, depth)]
            for q, folded in enumerate((first + second, first - second)):
                l_hi = folded.astype(jnp.bfloat16)
                l_lo = (folded - l_hi.astype(f32)).astype(jnp.bfloat16)
                table = table_ref[q, cols, :]
                t_hi = table.astype(jnp.bfloat16)
                t_lo = (table - t_hi.astype(f32)).astype(jnp.bfloat16)
                acc = jnp.dot(l_hi, t_hi, preferred_element_type=f32)
                acc = acc + jnp.dot(l_lo, t_hi, preferred_element_type=f32)
                acc = acc + jnp.dot(l_hi, t_lo, preferred_element_type=f32)
                out_ref[q] += acc
            return carry

        lax.fori_loop(0, half // depth, kstep, 0)


def band_spectra(voltages, window, table, frames, first_slot, n_slots):
    in_dev, length = voltages.shape
    frame_len = window.shape[1]
    half = frame_len // 2
    band = table.shape[2]
    block = 16
    rows = n_slots * in_dev
    kernel = functools.partial(taps_dft_kernel, first_slot=first_slot, n_slots=n_slots)
    return pl.pallas_call(
        kernel,
        out_shape=jax.ShapeDtypeStruct((2, rows, band), jnp.float32),
        grid=(in_dev // block,),
        in_specs=[
            pl.BlockSpec((block, length), lambda g: (g, 0)),
            pl.BlockSpec((TAPS, frame_len), lambda g: (0, 0)),
            pl.BlockSpec(memory_space=pl.ANY),
        ],
        out_specs=pl.BlockSpec((2, rows, band), lambda g: (0, 0, 0)),
        scratch_shapes=[
            pltpu.VMEM((rows, frame_len), jnp.float32),
            pltpu.VMEM((2, half, band), jnp.float32),
            pltpu.SemaphoreType.DMA((1,)),
        ],
        compiler_params=pltpu.CompilerParams(vmem_limit_bytes=48 * 1024 * 1024),
    )(voltages, window, table)


def on_device(voltages, gains):
    in_dev, length = voltages.shape
    band = gains.shape[2]
    half_band = band // 2
    frame_len = 2 * CHANNELS
    frames = length // frame_len
    n_time = lax.axis_size("tm")
    n_station = lax.axis_size("stn")
    all_inputs = in_dev * n_station
    history = TAPS - 1
    window = jnp.asarray(window_table(CHANNELS))
    table = band_tables(frame_len, band)

    raw_next = band_spectra(voltages, window, table, frames, frames, history)
    given = passed_along(raw_next, "tm", 1)
    raw = band_spectra(voltages, window, table, frames, 0, frames)
    raw = raw.at[:, : history * in_dev, :].add(given)
    raw = jnp.transpose(raw, (0, 2, 1))

    row = frames * in_dev
    raw = jnp.transpose(raw.reshape(2, 2, half_band, row), (1, 2, 0, 3))
    raw_re, raw_im = raw[0], raw[1]
    g = jnp.transpose(gains.reshape(2, in_dev, half_band, 2), (0, 2, 3, 1))
    g = jnp.tile(g, (1, 1, 1, frames))
    gain_re, gain_im = g[0], g[1]
    spec_re = gain_re * raw_re - gain_im * raw_im
    spec_im = gain_re * raw_im + gain_im * raw_re
    spectra = jnp.stack([spec_re, spec_im], axis=2).astype(jnp.bfloat16)
    spectra = spectra.reshape(n_time * n_station, 2 * row)
    spectra = lax.all_to_all(spectra, ("tm", "stn"), split_axis=0, concat_axis=0, tiled=True)
    spectra = spectra.reshape(n_time, n_station, 2, frames, in_dev)
    stacked = jnp.transpose(spectra, (2, 0, 3, 1, 4)).reshape(2, n_time * frames, all_inputs)
    flipped = jnp.concatenate([stacked[1], -stacked[0]], axis=0)
    stacked = stacked.reshape(2 * n_time * frames, all_inputs)
    both = jnp.concatenate([stacked, flipped], axis=1)
    vis = jnp.einsum("ki,kj->ij", both, stacked, preferred_element_type=jnp.float32)
    vis = vis * (1.0 / float(n_time * frames))
    return vis.reshape(1, 2, all_inputs, all_inputs)


def solution(mesh):
    in_specs = (P("stn", "tm"), P(None, "stn", None))
    out_specs = P(("tm", "stn"), None, None, None)
    return jax.shard_map(
        on_device, mesh=mesh, in_specs=in_specs, out_specs=out_specs, check_vma=False
    )
```

```python
import functools

import numpy as np

import jax
import jax.numpy as jnp
from jax import lax
from jax.experimental import pallas as pl
from jax.experimental.pallas import tpu as pltpu
from jax.sharding import PartitionSpec as P

CHANNELS = 4096
BAND_LOW = 1024
TAPS = 8


def passed_along(x, axis, by):
    devices = lax.axis_size(axis)
    pairs = [(i, i + by) for i in range(devices) if 0 <= i + by < devices]
    return lax.ppermute(x, axis, pairs)


def window_table(chans):
    frame_len = 2 * chans
    total_len = TAPS * frame_len
    positions = np.arange(total_len, dtype=np.float64)
    centred = (positions - (total_len - 1) / 2.0) / frame_len
    taper = np.sin(np.pi * (positions + 0.5) / total_len)
    shaped = np.sinc(centred) * taper * taper
    shaped = shaped / np.sqrt(np.sum(shaped * shaped))
    return shaped.reshape(TAPS, frame_len).astype(np.float32)


def split(x):
    hi = lax.reduce_precision(x, exponent_bits=8, mantissa_bits=7)
    lo = x - hi
    return hi.astype(jnp.bfloat16), lo.astype(jnp.bfloat16)


def band_tables(frame_len, band):
    half = band // 2
    n_b = 32
    n_a = frame_len // 2 // n_b
    q = jnp.arange(2, dtype=jnp.int32)[:, None, None]
    k = jnp.arange(band, dtype=jnp.int32)[None, None, :]
    chan = 2 * (k % half) + q
    imag_col = k >= half
    a = jnp.arange(n_a, dtype=jnp.int32)[None, :, None]
    b = jnp.arange(n_b, dtype=jnp.int32)[None, :, None]
    p_steps = n_a * 2
    tp = (2.0 * jnp.pi / p_steps) * ((a * chan) % p_steps).astype(jnp.float32)
    tq = (2.0 * jnp.pi / frame_len) * ((b * (BAND_LOW + chan)) % frame_len).astype(jnp.float32)
    pr, pi = jnp.cos(tp), -jnp.sin(tp)
    qr, qi = jnp.cos(tq), -jnp.sin(tq)
    b1 = jnp.where(imag_col, qi, qr)
    b2 = jnp.where(imag_col, qr, -qi)
    t = pr[:, :, None, :] * b1[:, None, :, :] + pi[:, :, None, :] * b2[:, None, :, :]
    return t.reshape(2, n_a * n_b, band)


def taps_dft_kernel(x_ref, w_ref, table_hbm, out_ref, lhs_ref, table_ref, sem, *, first_slot, n_slots):
    step = pl.program_id(0)
    steps = pl.num_programs(0)
    block = x_ref.shape[0]
    inputs = block * steps
    frame_len = w_ref.shape[1]
    half = frame_len // 2
    frames = x_ref.shape[1] // frame_len
    history = TAPS - 1
    lanes = 128
    copy_table = pltpu.make_async_copy(table_hbm, table_ref, sem.at[0])

    @pl.when(step == 0)
    def _():
        copy_table.start()

    row0 = pl.multiple_of(step * block, block)

    def chunk(j, carry):
        base = pl.multiple_of(j * lanes, lanes)
        for r0 in range(0, block, 8):
            inputs_at = pl.ds(r0, 8)
            xs = []
            ws = []
            for offset in (0, half):
                xs.append([x_ref[inputs_at, pl.ds(f * frame_len + offset + base, lanes)].astype(jnp.float32) for f in range(frames)])
                ws.append([w_ref[pl.ds(p, 1), pl.ds(offset + base, lanes)] for p in range(TAPS)])
            for slot in range(n_slots):
                s = first_slot + slot
                accs = []
                for part in range(2):
                    acc = None
                    for p in range(TAPS):
                        g = s + p - history
                        if 0 <= g < frames:
                            term = ws[part][p] * xs[part][g]
                            acc = term if acc is None else acc + term
                    accs.append(acc)
                rows = pl.ds(pl.multiple_of(slot * inputs + row0 + r0, 8), 8)
                lhs_ref[rows, pl.ds(base, lanes)] = accs[0]
                lhs_ref[rows, pl.ds(half + base, lanes)] = accs[1]
        return carry

    lax.fori_loop(0, half // lanes, chunk, 0)

    @pl.when(step == steps - 1)
    def _():
        copy_table.wait()
        depth = 1024
        f32 = jnp.float32
        out_ref[...] = jnp.zeros(out_ref.shape, f32)

        def kstep(kk, carry):
            k0 = pl.multiple_of(kk * depth, depth)
            cols = pl.ds(k0, depth)
            first = lhs_ref[:, cols]
            second = lhs_ref[:, pl.ds(half + k0, depth)]
            for q, folded in enumerate((first + second, first - second)):
                l_hi = folded.astype(jnp.bfloat16)
                l_lo = (folded - l_hi.astype(f32)).astype(jnp.bfloat16)
                table = table_ref[q, cols, :]
                t_hi = table.astype(jnp.bfloat16)
                t_lo = (table - t_hi.astype(f32)).astype(jnp.bfloat16)
                acc = jnp.dot(l_hi, t_hi, preferred_element_type=f32)
                acc = acc + jnp.dot(l_lo, t_hi, preferred_element_type=f32)
                acc = acc + jnp.dot(l_hi, t_lo, preferred_element_type=f32)
                out_ref[q] += acc
            return carry

        lax.fori_loop(0, half // depth, kstep, 0)


def band_spectra(voltages, window, table, frames, first_slot, n_slots):
    in_dev, length = voltages.shape
    frame_len = window.shape[1]
    half = frame_len // 2
    band = table.shape[2]
    block = 16
    rows = n_slots * in_dev
    kernel = functools.partial(taps_dft_kernel, first_slot=first_slot, n_slots=n_slots)
    return pl.pallas_call(
        kernel,
        out_shape=jax.ShapeDtypeStruct((2, rows, band), jnp.float32),
        grid=(in_dev // block,),
        in_specs=[
            pl.BlockSpec((block, length), lambda g: (g, 0)),
            pl.BlockSpec((TAPS, frame_len), lambda g: (0, 0)),
            pl.BlockSpec(memory_space=pl.ANY),
        ],
        out_specs=pl.BlockSpec((2, rows, band), lambda g: (0, 0, 0)),
        scratch_shapes=[
            pltpu.VMEM((rows, frame_len), jnp.float32),
            pltpu.VMEM((2, half, band), jnp.float32),
            pltpu.SemaphoreType.DMA((1,)),
        ],
        compiler_params=pltpu.CompilerParams(vmem_limit_bytes=48 * 1024 * 1024),
    )(voltages, window, table)


def on_device(voltages, gains):
    in_dev, length = voltages.shape
    band = gains.shape[2]
    half_band = band // 2
    frame_len = 2 * CHANNELS
    frames = length // frame_len
    n_time = lax.axis_size("tm")
    n_station = lax.axis_size("stn")
    all_inputs = in_dev * n_station
    history = TAPS - 1
    window = jnp.asarray(window_table(CHANNELS))
    table = band_tables(frame_len, band)

    raw_next = band_spectra(voltages, window, table, frames, frames, history)
    given = passed_along(raw_next, "tm", 1)
    raw = band_spectra(voltages, window, table, frames, 0, frames)
    raw = raw.at[:, : history * in_dev, :].add(given)
    raw = jnp.transpose(raw, (0, 2, 1))

    row = frames * in_dev
    raw = jnp.transpose(raw.reshape(2, 2, half_band, row), (1, 2, 0, 3))
    raw_re, raw_im = raw[0], raw[1]
    g = jnp.transpose(gains.reshape(2, in_dev, half_band, 2), (0, 2, 3, 1))
    g = jnp.tile(g, (1, 1, 1, frames))
    gain_re, gain_im = g[0], g[1]
    spec_re = gain_re * raw_re - gain_im * raw_im
    spec_im = gain_re * raw_im + gain_im * raw_re
    spectra = jnp.stack([spec_re, spec_im], axis=2).astype(jnp.bfloat16)
    spectra = spectra.reshape(n_time * n_station, 2 * row)
    spectra = lax.all_to_all(spectra, ("tm", "stn"), split_axis=0, concat_axis=0, tiled=True)
    spectra = spectra.reshape(n_time, n_station, 2, frames, in_dev)
    stacked = jnp.transpose(spectra, (2, 0, 3, 1, 4)).reshape(2, n_time * frames, all_inputs)
    flipped = jnp.concatenate([stacked[1], -stacked[0]], axis=0)
    stacked = stacked.reshape(2 * n_time * frames, all_inputs)
    both = jnp.concatenate([stacked, flipped], axis=1)
    vis = jnp.einsum("ki,kj->ij", both, stacked, preferred_element_type=jnp.float32)
    vis = vis * (1.0 / float(n_time * frames))
    return vis.reshape(1, 2, all_inputs, all_inputs)


def solution(mesh):
    in_specs = (P("stn", "tm"), P(None, "stn", None))
    out_specs = P(("tm", "stn"), None, None, None)
    return jax.shard_map(
        on_device, mesh=mesh, in_specs=in_specs, out_specs=out_specs, check_vma=False
    )
```

```python
import functools

import numpy as np

import jax
import jax.numpy as jnp
from jax import lax
from jax.experimental import pallas as pl
from jax.experimental.pallas import tpu as pltpu
from jax.sharding import PartitionSpec as P

CHANNELS = 4096
BAND_LOW = 1024
TAPS = 8


def passed_along(x, axis, by):
    devices = lax.axis_size(axis)
    pairs = [(i, i + by) for i in range(devices) if 0 <= i + by < devices]
    return lax.ppermute(x, axis, pairs)


def window_table(chans):
    frame_len = 2 * chans
    total_len = TAPS * frame_len
    positions = np.arange(total_len, dtype=np.float64)
    centred = (positions - (total_len - 1) / 2.0) / frame_len
    taper = np.sin(np.pi * (positions + 0.5) / total_len)
    shaped = np.sinc(centred) * taper * taper
    shaped = shaped / np.sqrt(np.sum(shaped * shaped))
    return shaped.reshape(TAPS, frame_len).astype(np.float32)


def split(x):
    hi = lax.reduce_precision(x, exponent_bits=8, mantissa_bits=7)
    lo = x - hi
    return hi.astype(jnp.bfloat16), lo.astype(jnp.bfloat16)


def band_tables(frame_len, band):
    half = band // 2
    n_b = 32
    n_a = frame_len // 2 // n_b
    q = jnp.arange(2, dtype=jnp.int32)[:, None, None]
    k = jnp.arange(band, dtype=jnp.int32)[None, None, :]
    chan = 2 * (k % half) + q
    imag_col = k >= half
    a = jnp.arange(n_a, dtype=jnp.int32)[None, :, None]
    b = jnp.arange(n_b, dtype=jnp.int32)[None, :, None]
    p_steps = n_a * 2
    tp = (2.0 * jnp.pi / p_steps) * ((a * chan) % p_steps).astype(jnp.float32)
    tq = (2.0 * jnp.pi / frame_len) * ((b * (BAND_LOW + chan)) % frame_len).astype(jnp.float32)
    pr, pi = jnp.cos(tp), -jnp.sin(tp)
    qr, qi = jnp.cos(tq), -jnp.sin(tq)
    b1 = jnp.where(imag_col, qi, qr)
    b2 = jnp.where(imag_col, qr, -qi)
    t = pr[:, :, None, :] * b1[:, None, :, :] + pi[:, :, None, :] * b2[:, None, :, :]
    return t.reshape(2, n_a * n_b, band)


def taps_dft_kernel(x_ref, w_ref, table_hbm, out_ref, lhs_ref, table_ref, sem, *, first_slot, n_slots):
    step = pl.program_id(0)
    steps = pl.num_programs(0)
    block = x_ref.shape[0]
    inputs = block * steps
    frame_len = w_ref.shape[1]
    half = frame_len // 2
    frames = x_ref.shape[1] // frame_len
    history = TAPS - 1
    lanes = 128
    copy_table = pltpu.make_async_copy(table_hbm, table_ref, sem.at[0])

    @pl.when(step == 0)
    def _():
        copy_table.start()

    row0 = pl.multiple_of(step * block, block)

    def chunk(j, carry):
        base = pl.multiple_of(j * lanes, lanes)
        for r0 in range(0, block, 8):
            inputs_at = pl.ds(r0, 8)
            xs = []
            ws = []
            for offset in (0, half):
                xs.append([x_ref[inputs_at, pl.ds(f * frame_len + offset + base, lanes)].astype(jnp.float32) for f in range(frames)])
                ws.append([w_ref[pl.ds(p, 1), pl.ds(offset + base, lanes)] for p in range(TAPS)])
            for slot in range(n_slots):
                s = first_slot + slot
                accs = []
                for part in range(2):
                    acc = None
                    for p in range(TAPS):
                        g = s + p - history
                        if 0 <= g < frames:
                            term = ws[part][p] * xs[part][g]
                            acc = term if acc is None else acc + term
                    accs.append(acc)
                rows = pl.ds(pl.multiple_of(slot * inputs + row0 + r0, 8), 8)
                lhs_ref[rows, pl.ds(base, lanes)] = accs[0]
                lhs_ref[rows, pl.ds(half + base, lanes)] = accs[1]
        return carry

    lax.fori_loop(0, half // lanes, chunk, 0)

    @pl.when(step == steps - 1)
    def _():
        copy_table.wait()
        depth = 2048
        f32 = jnp.float32
        out_ref[...] = jnp.zeros(out_ref.shape, f32)

        def kstep(kk, carry):
            k0 = pl.multiple_of(kk * depth, depth)
            cols = pl.ds(k0, depth)
            first = lhs_ref[:, cols]
            second = lhs_ref[:, pl.ds(half + k0, depth)]
            for q, folded in enumerate((first + second, first - second)):
                l_hi = folded.astype(jnp.bfloat16)
                l_lo = (folded - l_hi.astype(f32)).astype(jnp.bfloat16)
                table = table_ref[q, cols, :]
                t_hi = table.astype(jnp.bfloat16)
                t_lo = (table - t_hi.astype(f32)).astype(jnp.bfloat16)
                acc = jnp.dot(l_hi, t_hi, preferred_element_type=f32)
                acc = acc + jnp.dot(l_lo, t_hi, preferred_element_type=f32)
                acc = acc + jnp.dot(l_hi, t_lo, preferred_element_type=f32)
                out_ref[q] += acc
            return carry

        lax.fori_loop(0, half // depth, kstep, 0)


def band_spectra(voltages, window, table, frames, first_slot, n_slots):
    in_dev, length = voltages.shape
    frame_len = window.shape[1]
    half = frame_len // 2
    band = table.shape[2]
    block = 16
    rows = n_slots * in_dev
    kernel = functools.partial(taps_dft_kernel, first_slot=first_slot, n_slots=n_slots)
    return pl.pallas_call(
        kernel,
        out_shape=jax.ShapeDtypeStruct((2, rows, band), jnp.float32),
        grid=(in_dev // block,),
        in_specs=[
            pl.BlockSpec((block, length), lambda g: (g, 0)),
            pl.BlockSpec((TAPS, frame_len), lambda g: (0, 0)),
            pl.BlockSpec(memory_space=pl.ANY),
        ],
        out_specs=pl.BlockSpec((2, rows, band), lambda g: (0, 0, 0)),
        scratch_shapes=[
            pltpu.VMEM((rows, frame_len), jnp.float32),
            pltpu.VMEM((2, half, band), jnp.float32),
            pltpu.SemaphoreType.DMA((1,)),
        ],
        compiler_params=pltpu.CompilerParams(vmem_limit_bytes=48 * 1024 * 1024),
    )(voltages, window, table)


def on_device(voltages, gains):
    in_dev, length = voltages.shape
    band = gains.shape[2]
    half_band = band // 2
    frame_len = 2 * CHANNELS
    frames = length // frame_len
    n_time = lax.axis_size("tm")
    n_station = lax.axis_size("stn")
    all_inputs = in_dev * n_station
    history = TAPS - 1
    window = jnp.asarray(window_table(CHANNELS))
    table = band_tables(frame_len, band)

    raw_next = band_spectra(voltages, window, table, frames, frames, history)
    given = passed_along(raw_next, "tm", 1)
    raw = band_spectra(voltages, window, table, frames, 0, frames)
    raw = raw.at[:, : history * in_dev, :].add(given)
    raw = jnp.transpose(raw, (0, 2, 1))

    row = frames * in_dev
    raw = jnp.transpose(raw.reshape(2, 2, half_band, row), (1, 2, 0, 3))
    raw_re, raw_im = raw[0], raw[1]
    g = jnp.transpose(gains.reshape(2, in_dev, half_band, 2), (0, 2, 3, 1))
    g = jnp.tile(g, (1, 1, 1, frames))
    gain_re, gain_im = g[0], g[1]
    spec_re = gain_re * raw_re - gain_im * raw_im
    spec_im = gain_re * raw_im + gain_im * raw_re
    spectra = jnp.stack([spec_re, spec_im], axis=2).astype(jnp.bfloat16)
    spectra = spectra.reshape(n_time * n_station, 2 * row)
    spectra = lax.all_to_all(spectra, ("tm", "stn"), split_axis=0, concat_axis=0, tiled=True)
    spectra = spectra.reshape(n_time, n_station, 2, frames, in_dev)
    stacked = jnp.transpose(spectra, (2, 0, 3, 1, 4)).reshape(2, n_time * frames, all_inputs)
    flipped = jnp.concatenate([stacked[1], -stacked[0]], axis=0)
    stacked = stacked.reshape(2 * n_time * frames, all_inputs)
    both = jnp.concatenate([stacked, flipped], axis=1)
    vis = jnp.einsum("ki,kj->ij", both, stacked, preferred_element_type=jnp.float32)
    vis = vis * (1.0 / float(n_time * frames))
    return vis.reshape(1, 2, all_inputs, all_inputs)


def solution(mesh):
    in_specs = (P("stn", "tm"), P(None, "stn", None))
    out_specs = P(("tm", "stn"), None, None, None)
    return jax.shard_map(
        on_device, mesh=mesh, in_specs=in_specs, out_specs=out_specs, check_vma=False
    )
```

```python
import functools

import numpy as np

import jax
import jax.numpy as jnp
from jax import lax
from jax.experimental import pallas as pl
from jax.experimental.pallas import tpu as pltpu
from jax.sharding import PartitionSpec as P

CHANNELS = 4096
BAND_LOW = 1024
TAPS = 8


def passed_along(x, axis, by):
    devices = lax.axis_size(axis)
    pairs = [(i, i + by) for i in range(devices) if 0 <= i + by < devices]
    return lax.ppermute(x, axis, pairs)


def window_table(chans):
    frame_len = 2 * chans
    total_len = TAPS * frame_len
    positions = np.arange(total_len, dtype=np.float64)
    centred = (positions - (total_len - 1) / 2.0) / frame_len
    taper = np.sin(np.pi * (positions + 0.5) / total_len)
    shaped = np.sinc(centred) * taper * taper
    shaped = shaped / np.sqrt(np.sum(shaped * shaped))
    return shaped.reshape(TAPS, frame_len).astype(np.float32)


def split(x):
    hi = lax.reduce_precision(x, exponent_bits=8, mantissa_bits=7)
    lo = x - hi
    return hi.astype(jnp.bfloat16), lo.astype(jnp.bfloat16)


def band_tables(frame_len, band):
    half = band // 2
    n_b = 32
    n_a = frame_len // 2 // n_b
    q = jnp.arange(2, dtype=jnp.int32)[:, None, None]
    k = jnp.arange(band, dtype=jnp.int32)[None, None, :]
    chan = 2 * (k % half) + q
    imag_col = k >= half
    a = jnp.arange(n_a, dtype=jnp.int32)[None, :, None]
    b = jnp.arange(n_b, dtype=jnp.int32)[None, :, None]
    p_steps = n_a * 2
    tp = (2.0 * jnp.pi / p_steps) * ((a * chan) % p_steps).astype(jnp.float32)
    tq = (2.0 * jnp.pi / frame_len) * ((b * (BAND_LOW + chan)) % frame_len).astype(jnp.float32)
    pr, pi = jnp.cos(tp), -jnp.sin(tp)
    qr, qi = jnp.cos(tq), -jnp.sin(tq)
    b1 = jnp.where(imag_col, qi, qr)
    b2 = jnp.where(imag_col, qr, -qi)
    t = pr[:, :, None, :] * b1[:, None, :, :] + pi[:, :, None, :] * b2[:, None, :, :]
    return t.reshape(2, n_a * n_b, band)


def taps_dft_kernel(x_ref, w_ref, table_hbm, out_ref, lhs_ref, table_ref, sem, *, first_slot, n_slots):
    step = pl.program_id(0)
    steps = pl.num_programs(0)
    block = x_ref.shape[0]
    inputs = block * steps
    frame_len = w_ref.shape[1]
    half = frame_len // 2
    frames = x_ref.shape[1] // frame_len
    history = TAPS - 1
    lanes = 128
    copy_table = pltpu.make_async_copy(table_hbm, table_ref, sem.at[0])

    @pl.when(step == 0)
    def _():
        copy_table.start()

    row0 = pl.multiple_of(step * block, block)

    def chunk(j, carry):
        base = pl.multiple_of(j * lanes, lanes)
        for r0 in range(0, block, 8):
            inputs_at = pl.ds(r0, 8)
            xs = []
            ws = []
            for offset in (0, half):
                xs.append([x_ref[inputs_at, pl.ds(f * frame_len + offset + base, lanes)].astype(jnp.float32) for f in range(frames)])
                ws.append([w_ref[pl.ds(p, 1), pl.ds(offset + base, lanes)] for p in range(TAPS)])
            for slot in range(n_slots):
                s = first_slot + slot
                accs = []
                for part in range(2):
                    acc = None
                    for p in range(TAPS):
                        g = s + p - history
                        if 0 <= g < frames:
                            term = ws[part][p] * xs[part][g]
                            acc = term if acc is None else acc + term
                    accs.append(acc)
                rows = pl.ds(pl.multiple_of(slot * inputs + row0 + r0, 8), 8)
                lhs_ref[rows, pl.ds(base, lanes)] = accs[0]
                lhs_ref[rows, pl.ds(half + base, lanes)] = accs[1]
        return carry

    lax.fori_loop(0, half // lanes, chunk, 0)

    @pl.when(step == steps - 1)
    def _():
        copy_table.wait()
        depth = 4096
        f32 = jnp.float32
        out_ref[...] = jnp.zeros(out_ref.shape, f32)

        def kstep(kk, carry):
            k0 = pl.multiple_of(kk * depth, depth)
            cols = pl.ds(k0, depth)
            first = lhs_ref[:, cols]
            second = lhs_ref[:, pl.ds(half + k0, depth)]
            for q, folded in enumerate((first + second, first - second)):
                l_hi = folded.astype(jnp.bfloat16)
                l_lo = (folded - l_hi.astype(f32)).astype(jnp.bfloat16)
                table = table_ref[q, cols, :]
                t_hi = table.astype(jnp.bfloat16)
                t_lo = (table - t_hi.astype(f32)).astype(jnp.bfloat16)
                acc = jnp.dot(l_hi, t_hi, preferred_element_type=f32)
                acc = acc + jnp.dot(l_lo, t_hi, preferred_element_type=f32)
                acc = acc + jnp.dot(l_hi, t_lo, preferred_element_type=f32)
                out_ref[q] += acc
            return carry

        lax.fori_loop(0, half // depth, kstep, 0)


def band_spectra(voltages, window, table, frames, first_slot, n_slots):
    in_dev, length = voltages.shape
    frame_len = window.shape[1]
    half = frame_len // 2
    band = table.shape[2]
    block = 16
    rows = n_slots * in_dev
    kernel = functools.partial(taps_dft_kernel, first_slot=first_slot, n_slots=n_slots)
    return pl.pallas_call(
        kernel,
        out_shape=jax.ShapeDtypeStruct((2, rows, band), jnp.float32),
        grid=(in_dev // block,),
        in_specs=[
            pl.BlockSpec((block, length), lambda g: (g, 0)),
            pl.BlockSpec((TAPS, frame_len), lambda g: (0, 0)),
            pl.BlockSpec(memory_space=pl.ANY),
        ],
        out_specs=pl.BlockSpec((2, rows, band), lambda g: (0, 0, 0)),
        scratch_shapes=[
            pltpu.VMEM((rows, frame_len), jnp.float32),
            pltpu.VMEM((2, half, band), jnp.float32),
            pltpu.SemaphoreType.DMA((1,)),
        ],
        compiler_params=pltpu.CompilerParams(vmem_limit_bytes=48 * 1024 * 1024),
    )(voltages, window, table)


def on_device(voltages, gains):
    in_dev, length = voltages.shape
    band = gains.shape[2]
    half_band = band // 2
    frame_len = 2 * CHANNELS
    frames = length // frame_len
    n_time = lax.axis_size("tm")
    n_station = lax.axis_size("stn")
    all_inputs = in_dev * n_station
    history = TAPS - 1
    window = jnp.asarray(window_table(CHANNELS))
    table = band_tables(frame_len, band)

    raw_next = band_spectra(voltages, window, table, frames, frames, history)
    given = passed_along(raw_next, "tm", 1)
    raw = band_spectra(voltages, window, table, frames, 0, frames)
    raw = raw.at[:, : history * in_dev, :].add(given)
    raw = jnp.transpose(raw, (0, 2, 1))

    row = frames * in_dev
    raw = jnp.transpose(raw.reshape(2, 2, half_band, row), (1, 2, 0, 3))
    raw_re, raw_im = raw[0], raw[1]
    g = jnp.transpose(gains.reshape(2, in_dev, half_band, 2), (0, 2, 3, 1))
    g = jnp.tile(g, (1, 1, 1, frames))
    gain_re, gain_im = g[0], g[1]
    spec_re = gain_re * raw_re - gain_im * raw_im
    spec_im = gain_re * raw_im + gain_im * raw_re
    spectra = jnp.stack([spec_re, spec_im], axis=2).astype(jnp.bfloat16)
    spectra = spectra.reshape(n_time * n_station, 2 * row)
    spectra = lax.all_to_all(spectra, ("tm", "stn"), split_axis=0, concat_axis=0, tiled=True)
    spectra = spectra.reshape(n_time, n_station, 2, frames, in_dev)
    stacked = jnp.transpose(spectra, (2, 0, 3, 1, 4)).reshape(2, n_time * frames, all_inputs)
    flipped = jnp.concatenate([stacked[1], -stacked[0]], axis=0)
    stacked = stacked.reshape(2 * n_time * frames, all_inputs)
    both = jnp.concatenate([stacked, flipped], axis=1)
    vis = jnp.einsum("ki,kj->ij", both, stacked, preferred_element_type=jnp.float32)
    vis = vis * (1.0 / float(n_time * frames))
    return vis.reshape(1, 2, all_inputs, all_inputs)


def solution(mesh):
    in_specs = (P("stn", "tm"), P(None, "stn", None))
    out_specs = P(("tm", "stn"), None, None, None)
    return jax.shard_map(
        on_device, mesh=mesh, in_specs=in_specs, out_specs=out_specs, check_vma=False
    )
```
